256 devices in a mesh: child: 64 (over x, z_hi, y), tensor: 4 (over z_lo, core).
Axes of the slice: x: 4, y: 4, z: 8 (z_hi: 4, z_lo: 2; z = z_hi * 2 + z_lo), core: 2. Of those that a mesh axis runs over, the one named last changes fastest.
Arguments:
- tokens: bfloat16 [32768, 5120], P('child'), may hold values from -28 to 28
- episode: int32 [64, 512], P('child'), may hold values from 0 to 3, never falling along the last dimension, each value on 1 to 256 neighbouring positions
- parent_index: int32 [64], replicated, may hold values from 0 to 1
- mutation_seed: int32 [64], P('child'), may hold values from 0 to 1073741823
- elite_project: bfloat16 [2, 5120, 4, 896], P(None, 'child', 'tensor'), may hold values from -0.078125 to 0.078125
- elite_output: bfloat16 [2, 5120, 4, 640], P(None, 'child', 'tensor'), may hold values from -0.23925781 to 0.23925781
- elite_bias: float32 [2, 4, 896], P(None, 'tensor'), may hold values from -1.2 to 1.2
Outputs:
- attended: bfloat16 [32768, 5120], P('child', 'tensor')
The draws below stay inside these ranges and needn't reach their ends.
Inputs may be any that keep to these rules, and one draw needn't show every extreme that they name: Along each member's rows the episode numbers never fall; each of the 4 episodes has 1 to 256 rows, and some episode has exactly 256.
All inputs are finite; a program needn't handle non-finite values.
Results may differ from the reference program's by a relative error of at most 0.007.
The reference program's roundings to bfloat16 on the way count: a program that leaves them out, or rounds other values in their place, can miss the bound.
Values may be sent and summed in bfloat16 or wider, within the bound.
No kernel may reach another device: no remote copies, remote signals or barrier semaphores. Data moves between devices by JAX's collectives and lax.ppermute only.
A program may use at most 128 MiB of HBM per device.

```python
import math
from functools import partial
import jax
import jax.numpy as jnp
import numpy as np
from jax import lax

D = 5120
HEAD_DIM = 128
KV_HEADS = 4
GROUP = 5
ELITES = 2
EPISODES = 4
ROWS = 512
MEMBERS = 64
IN_COLUMNS = 896
OUT_COLUMNS = 640


def draw_tokens(key, part):
    shape = (MEMBERS * ROWS, D)
    return jnp.clip(jax.random.normal(key, shape, jnp.float32), -6.0, 6.0).astype(jnp.bfloat16)


def place_ends(drawn, rng, low, top_value):
    longest = drawn.shape.index(max(drawn.shape))
    spots = []
    for shift in (0, 1):
        where = [jax.random.randint(jax.random.fold_in(rng, axis), (), 0, length) for axis, length in enumerate(drawn.shape)]
        where[longest] = (where[longest] + shift) % drawn.shape[longest]
        spots.append(tuple(where))
    return drawn.at[spots[0]].set(low).at[spots[1]].set(top_value)


def block_levels(key, extent, pieces, smallest, high):
    factor_of, own = 1.0, jax.random.fold_in(key, 6)
    for dim, parts in pieces:
        heights = jnp.exp(jax.random.uniform(jax.random.fold_in(own, dim), (parts,), jnp.float32, smallest / len(pieces), high / len(pieces)))
        factor_of = factor_of * jnp.repeat(heights, extent[dim] // parts).reshape([-1 if axis == dim else 1 for axis in range(len(extent))])
    return factor_of


def profile(number_of, total, reach, slope):
    portions = [(1 << 20) // math.isqrt(standing ** slope) + 1 for standing in range(2, number_of + 1)]
    surplus, given = total - reach - (number_of - 1), [1] * (number_of - 1)
    while surplus > 0:
        movable = [i for i in range(number_of - 1) if given[i] < reach]
        mass, remaining = sum([portions[i] for i in movable]), surplus
        for i in movable:
            more = min(reach - given[i], max(1, remaining * portions[i] // mass), surplus)
            given[i] = given[i] + more
            surplus = surplus - more
    return np.array([reach] + given)


def ragged_sizes(key, amount, total, reach, slope):
    if amount == 2:
        one = jax.random.randint(key, (), max(1, total - reach), min(reach, total - 1) + 1)
        return jnp.stack([one, total - one])
    sizes = jnp.asarray(profile(amount, total, reach, slope), jnp.int32)
    pairs = (amount - 1) // 2
    source_of, sink = sizes[1:1 + 2 * pairs:2], sizes[2:2 + 2 * pairs:2]
    margin = jnp.minimum(source_of - 1, reach - sink)
    passed = jax.random.randint(jax.random.fold_in(key, 1), (pairs,), 0, 1 << 20) % (margin + 1)
    sizes = sizes.at[1:1 + 2 * pairs:2].set(source_of - passed).at[2:2 + 2 * pairs:2].set(sink + passed)
    return sizes[jax.random.permutation(jax.random.fold_in(key, 2), amount)]


def normal_values(rng, shape, scale, bound, pieces=(), kind=jnp.bfloat16):
    entries = scale * jax.random.normal(rng, shape, jnp.float32)
    if pieces:
        entries = entries * block_levels(rng, shape, pieces, -0.22, 0.18)
    return jnp.clip(entries, -bound, bound).astype(kind)


def setup_inputs(seed: int = 0) -> dict:
    key_of = jax.random.split(jax.random.key(seed), 8)
    return {
        "tokens": draw_tokens(jax.random.fold_in(key_of[7], 71), 0),
        "episode": jax.vmap(lambda own: jnp.searchsorted(jnp.cumsum(ragged_sizes(own, EPISODES, ROWS, ROWS // 2, 0)), jnp.arange(ROWS), side="right"))(jax.random.split(key_of[1], MEMBERS)).reshape((MEMBERS, ROWS)).astype(jnp.int32),
        "parent_index": place_ends(jax.random.randint(key_of[2], (MEMBERS,), 0, ELITES), jax.random.fold_in(key_of[2], 1), 0, ELITES - 1).astype(jnp.int32),
        "mutation_seed": place_ends(jax.random.randint(key_of[3], (MEMBERS,), 0, 1073741824), jax.random.fold_in(key_of[3], 1), 0, 1073741823).astype(jnp.int32),
        "elite_project": normal_values(key_of[4], (ELITES, D, KV_HEADS, IN_COLUMNS), D ** -0.5, 0.078125, ((1, 64), (2, 4))),
        "elite_output": normal_values(key_of[5], (ELITES, D, KV_HEADS, OUT_COLUMNS), 0.04, 0.23925781, ((1, 64), (2, 4))),
        "elite_bias": normal_values(key_of[6], (ELITES, KV_HEADS, IN_COLUMNS), 0.2, 1.2, ((1, 4),), jnp.float32),
    }


MUTATION = 0.25
BIAS_MUTATION = 0.05
ROPE_BASE = 1000000.0
NOISE_SPREAD = 147.80054

def mix_hash(seed_value, counter):
    hashed = counter + seed_value * jnp.int32(-1640531535)
    hashed = hashed ^ lax.shift_right_logical(hashed, jnp.full_like(hashed, 16))
    hashed = hashed * jnp.int32(-2048144789)
    hashed = hashed ^ lax.shift_right_logical(hashed, jnp.full_like(hashed, 13))
    hashed = hashed * jnp.int32(-1028477387)
    return hashed ^ lax.shift_right_logical(hashed, jnp.full_like(hashed, 16))

def gaussian(seed_value, counter):
    hashed = mix_hash(seed_value, counter)
    summed = jnp.bitwise_and(hashed, 255)
    summed = summed + jnp.bitwise_and(lax.shift_right_logical(hashed, jnp.full_like(hashed, 8)), 255)
    summed = summed + jnp.bitwise_and(lax.shift_right_logical(hashed, jnp.full_like(hashed, 16)), 255)
    summed = summed + lax.shift_right_logical(hashed, jnp.full_like(hashed, 24))
    return (summed - 510).astype(jnp.float32) / NOISE_SPREAD

def rotary(vectors, cosine, sine_table):
    half_dim = vectors.shape[-1] // 2
    first_half = vectors[..., :half_dim]
    second_half = vectors[..., half_dim:]
    return jnp.concatenate([first_half * cosine - second_half * sine_table, second_half * cosine + first_half * sine_table], axis=-1)

def episode_tables(episode_row):
    count_rows = episode_row.shape[0]
    same_episode = episode_row[:, None] == episode_row[None, :]
    earlier = lax.optimization_barrier(jnp.sum((episode_row[None, :] < episode_row[:, None]).astype(jnp.int32), axis=1))
    position = jnp.arange(count_rows, dtype=jnp.int32) - earlier
    causal = jnp.arange(count_rows)[None, :] <= jnp.arange(count_rows)[:, None]
    allowed = same_episode & causal
    frequency = jnp.exp(jnp.arange(0, HEAD_DIM, 2).astype(jnp.float32) * (-math.log(ROPE_BASE) / HEAD_DIM))
    angles = position.astype(jnp.float32)[:, None] * frequency[None, :]
    return (allowed, jnp.cos(angles), jnp.sin(angles))

def one_member(elite_project, elite_output, elite_bias, member_tokens, member_episode, parent, seed_value):
    row_ids = jnp.arange(D, dtype=jnp.int32)[:, None, None]
    group_ids = jnp.arange(KV_HEADS, dtype=jnp.int32)[None, :, None]
    counter_in = (row_ids * KV_HEADS + group_ids) * IN_COLUMNS + jnp.arange(IN_COLUMNS, dtype=jnp.int32)[None, None, :]
    child_in = (elite_project[parent].astype(jnp.float32) + MUTATION / math.sqrt(D) * gaussian(seed_value, counter_in)).astype(jnp.bfloat16)
    out_base = D * KV_HEADS * IN_COLUMNS
    counter_out = out_base + (row_ids * KV_HEADS + group_ids) * OUT_COLUMNS + jnp.arange(OUT_COLUMNS, dtype=jnp.int32)[None, None, :]
    child_out = (elite_output[parent].astype(jnp.float32) + MUTATION / math.sqrt(KV_HEADS * GROUP * HEAD_DIM) * gaussian(seed_value, counter_out)).astype(jnp.bfloat16)
    bias_base = out_base + D * KV_HEADS * OUT_COLUMNS
    counter_bias = bias_base + jnp.arange(KV_HEADS, dtype=jnp.int32)[:, None] * IN_COLUMNS + jnp.arange(IN_COLUMNS, dtype=jnp.int32)[None, :]
    child_bias = elite_bias[parent] + BIAS_MUTATION * gaussian(seed_value, counter_bias)
    projected = jnp.dot(member_tokens, child_in.reshape(D, KV_HEADS * IN_COLUMNS), preferred_element_type=jnp.float32)
    projected = projected.reshape(ROWS, KV_HEADS, IN_COLUMNS) + child_bias[None]
    allowed, cosine, sine_table = episode_tables(member_episode)
    query_part = projected[:, :, :GROUP * HEAD_DIM].reshape(ROWS, KV_HEADS, GROUP, HEAD_DIM)
    key_part = projected[:, :, GROUP * HEAD_DIM:(GROUP + 1) * HEAD_DIM]
    value_part = projected[:, :, (GROUP + 1) * HEAD_DIM:]
    queries = rotary(query_part, cosine[:, None, None, :], sine_table[:, None, None, :]).astype(jnp.bfloat16)
    key_rows = rotary(key_part, cosine[:, None, :], sine_table[:, None, :]).astype(jnp.bfloat16)
    values = value_part.astype(jnp.bfloat16)
    scores = jnp.einsum('rgqh,sgh->gqrs', queries.astype(jnp.float32), key_rows.astype(jnp.float32)) * (1.0 / math.sqrt(HEAD_DIM))
    masked = jnp.where(allowed[None, None], scores, -jnp.inf)
    row_max = lax.optimization_barrier(jnp.max(masked, axis=-1, keepdims=True))
    weights = jnp.exp(masked - row_max)
    probability = (weights / lax.optimization_barrier(jnp.sum(weights, axis=-1, keepdims=True))).astype(jnp.bfloat16)
    context = jnp.einsum('gqrs,sgh->rgqh', probability.astype(jnp.float32), values.astype(jnp.float32)).astype(jnp.bfloat16)
    context = context.reshape(ROWS, KV_HEADS * OUT_COLUMNS)
    result = jnp.dot(context, child_out.reshape(D, KV_HEADS * OUT_COLUMNS).T, preferred_element_type=jnp.float32)
    return result.astype(jnp.bfloat16)

def reference(tokens, episode, parent_index, mutation_seed, elite_project, elite_output, elite_bias):
    stacked = tokens.reshape(MEMBERS, ROWS, D)
    member_fn = partial(one_member, elite_project, elite_output, elite_bias)
    results = lax.map(lambda packed: member_fn(*packed), (stacked, episode, parent_index, mutation_seed))
    return results.reshape(MEMBERS * ROWS, D)
```

```python
import math

import jax
import jax.numpy as jnp
from jax import lax
from jax.sharding import PartitionSpec as P

D = 5120
HEAD_DIM = 128
KV_HEADS = 4
GROUP = 5


MUTATION = 0.25
BIAS_MUTATION = 0.05
ROPE_BASE = 1000000.0
NOISE_SPREAD = 147.80054


def mix_hash(seed_value, counter):
    hashed = counter + seed_value * jnp.int32(-1640531535)
    hashed = hashed ^ lax.shift_right_logical(hashed, jnp.full_like(hashed, 16))
    hashed = hashed * jnp.int32(-2048144789)
    hashed = hashed ^ lax.shift_right_logical(hashed, jnp.full_like(hashed, 13))
    hashed = hashed * jnp.int32(-1028477387)
    return hashed ^ lax.shift_right_logical(hashed, jnp.full_like(hashed, 16))


def gaussian(seed_value, counter):
    hashed = mix_hash(seed_value, counter)
    summed = jnp.bitwise_and(hashed, 255)
    summed = summed + jnp.bitwise_and(
        lax.shift_right_logical(hashed, jnp.full_like(hashed, 8)), 255
    )
    summed = summed + jnp.bitwise_and(
        lax.shift_right_logical(hashed, jnp.full_like(hashed, 16)), 255
    )
    summed = summed + lax.shift_right_logical(hashed, jnp.full_like(hashed, 24))
    return (summed - 510).astype(jnp.float32) / NOISE_SPREAD


def counter_grid(row_ids, group_ids, width, base):
    column_ids = jnp.arange(width, dtype=jnp.int32)
    return (
        base
        + (row_ids[:, None, None] * KV_HEADS + group_ids[None, :, None]) * width
        + column_ids[None, None, :]
    )


def rotary(vectors, cosine, sine_table):
    half_dim = vectors.shape[-1] // 2
    first_half = vectors[..., :half_dim]
    second_half = vectors[..., half_dim:]
    return jnp.concatenate(
        [
            first_half * cosine - second_half * sine_table,
            second_half * cosine + first_half * sine_table,
        ],
        axis=-1,
    )


def episode_tables(episode_row):
    count_rows = episode_row.shape[0]
    same_episode = episode_row[:, None] == episode_row[None, :]
    earlier = jnp.sum((episode_row[None, :] < episode_row[:, None]).astype(jnp.int32), axis=1)
    position = jnp.arange(count_rows, dtype=jnp.int32) - earlier
    causal = jnp.arange(count_rows)[None, :] <= jnp.arange(count_rows)[:, None]
    allowed = same_episode & causal
    frequency = jnp.exp(
        jnp.arange(0, HEAD_DIM, 2).astype(jnp.float32) * (-math.log(ROPE_BASE) / HEAD_DIM)
    )
    angles = position.astype(jnp.float32)[:, None] * frequency[None, :]
    return (allowed, jnp.cos(angles), jnp.sin(angles))


def on_device(
    tokens, episode, parent_index, mutation_seed, elite_project, elite_output, elite_bias
):
    child_rank = lax.axis_index("child")
    tensor_rank = lax.axis_index("tensor")
    kv_local = elite_project.shape[2]
    width_in = elite_project.shape[3]
    width_out = elite_output.shape[3]
    count_rows = tokens.shape[0]
    group_ids = tensor_rank * kv_local + jnp.arange(kv_local, dtype=jnp.int32)
    scale_in = MUTATION / math.sqrt(D)
    scale_out = MUTATION / math.sqrt(KV_HEADS * GROUP * HEAD_DIM)
    out_base = D * KV_HEADS * width_in
    bias_base = out_base + D * KV_HEADS * width_out
    own_seed = mutation_seed[0]
    parent = parent_index[child_rank]
    gathered_in = lax.all_gather(elite_project, "child", axis=1, tiled=True)
    gathered_out = lax.all_gather(elite_output, "child", axis=1, tiled=True)
    arrived_in = lax.dynamic_index_in_dim(gathered_in, parent, 0, keepdims=False)
    arrived_out = lax.dynamic_index_in_dim(gathered_out, parent, 0, keepdims=False)
    every_row = jnp.arange(D, dtype=jnp.int32)
    child_in = (
        arrived_in.astype(jnp.float32)
        + scale_in * gaussian(own_seed, counter_grid(every_row, group_ids, width_in, 0))
    ).astype(jnp.bfloat16)
    child_out = (
        arrived_out.astype(jnp.float32)
        + scale_out * gaussian(own_seed, counter_grid(every_row, group_ids, width_out, out_base))
    ).astype(jnp.bfloat16)
    counter_bias = (
        bias_base + group_ids[:, None] * width_in + jnp.arange(width_in, dtype=jnp.int32)[None, :]
    )
    child_bias = elite_bias[parent] + BIAS_MUTATION * gaussian(own_seed, counter_bias)
    projected = (
        jnp.einsum("rd,dgc->rgc", tokens, child_in, preferred_element_type=jnp.float32)
        + child_bias[None]
    )
    allowed, cosine, sine_table = episode_tables(episode[0])
    query_part = projected[:, :, : GROUP * HEAD_DIM].reshape(count_rows, kv_local, GROUP, HEAD_DIM)
    key_part = projected[:, :, GROUP * HEAD_DIM : (GROUP + 1) * HEAD_DIM]
    value_part = projected[:, :, (GROUP + 1) * HEAD_DIM :]
    queries = rotary(query_part, cosine[:, None, None, :], sine_table[:, None, None, :]).astype(
        jnp.bfloat16
    )
    key_rows = rotary(key_part, cosine[:, None, :], sine_table[:, None, :]).astype(jnp.bfloat16)
    values = value_part.astype(jnp.bfloat16)
    scores = jnp.einsum("rgqh,sgh->gqrs", queries, key_rows, preferred_element_type=jnp.float32) * (
        1.0 / math.sqrt(HEAD_DIM)
    )
    masked = jnp.where(allowed[None, None], scores, -jnp.inf)
    row_max = jnp.max(masked, axis=-1, keepdims=True)
    weights = jnp.exp(masked - row_max)
    probability = (weights / jnp.sum(weights, axis=-1, keepdims=True)).astype(jnp.bfloat16)
    context = jnp.einsum(
        "gqrs,sgh->rgqh", probability, values, preferred_element_type=jnp.float32
    ).astype(jnp.bfloat16)
    context = context.reshape(count_rows, kv_local, width_out)
    summed = lax.psum_scatter(
        jnp.einsum("dgc,rgc->dr", child_out, context, preferred_element_type=jnp.float32),
        "tensor",
        scatter_dimension=0,
        tiled=True,
    )
    return summed.T.astype(jnp.bfloat16)


def solution(mesh):
    in_specs = (
        P("child", None),
        P("child", None),
        P(),
        P("child"),
        P(None, "child", "tensor", None),
        P(None, "child", "tensor", None),
        P(None, "tensor", None),
    )
    out_specs = P("child", "tensor")
    return jax.shard_map(
        on_device, mesh=mesh, in_specs=in_specs, out_specs=out_specs, check_vma=False
    )
```

```python
import math

import jax
import jax.numpy as jnp
from jax import lax
from jax.sharding import PartitionSpec as P

D = 5120
HEAD_DIM = 128
KV_HEADS = 4
GROUP = 5


MUTATION = 0.25
BIAS_MUTATION = 0.05
ROPE_BASE = 1000000.0
NOISE_SPREAD = 147.80054


def mix_hash(seed_value, counter):
    hashed = counter + seed_value * jnp.int32(-1640531535)
    hashed = hashed ^ lax.shift_right_logical(hashed, jnp.full_like(hashed, 16))
    hashed = hashed * jnp.int32(-2048144789)
    hashed = hashed ^ lax.shift_right_logical(hashed, jnp.full_like(hashed, 13))
    hashed = hashed * jnp.int32(-1028477387)
    return hashed ^ lax.shift_right_logical(hashed, jnp.full_like(hashed, 16))


def gaussian(seed_value, counter):
    hashed = mix_hash(seed_value, counter)
    summed = jnp.bitwise_and(hashed, 255)
    summed = summed + jnp.bitwise_and(
        lax.shift_right_logical(hashed, jnp.full_like(hashed, 8)), 255
    )
    summed = summed + jnp.bitwise_and(
        lax.shift_right_logical(hashed, jnp.full_like(hashed, 16)), 255
    )
    summed = summed + lax.shift_right_logical(hashed, jnp.full_like(hashed, 24))
    return (summed - 510).astype(jnp.float32) / NOISE_SPREAD


def counter_grid(row_ids, group_ids, width, base):
    column_ids = jnp.arange(width, dtype=jnp.int32)
    return (
        base
        + (row_ids[:, None, None] * KV_HEADS + group_ids[None, :, None]) * width
        + column_ids[None, None, :]
    )


def rotary(vectors, cosine, sine_table):
    half_dim = vectors.shape[-1] // 2
    first_half = vectors[..., :half_dim]
    second_half = vectors[..., half_dim:]
    return jnp.concatenate(
        [
            first_half * cosine - second_half * sine_table,
            second_half * cosine + first_half * sine_table,
        ],
        axis=-1,
    )


def episode_tables(episode_row):
    count_rows = episode_row.shape[0]
    same_episode = episode_row[:, None] == episode_row[None, :]
    earlier = jnp.sum((episode_row[None, :] < episode_row[:, None]).astype(jnp.int32), axis=1)
    position = jnp.arange(count_rows, dtype=jnp.int32) - earlier
    causal = jnp.arange(count_rows)[None, :] <= jnp.arange(count_rows)[:, None]
    allowed = same_episode & causal
    frequency = jnp.exp(
        jnp.arange(0, HEAD_DIM, 2).astype(jnp.float32) * (-math.log(ROPE_BASE) / HEAD_DIM)
    )
    angles = position.astype(jnp.float32)[:, None] * frequency[None, :]
    return (allowed, jnp.cos(angles), jnp.sin(angles))


def output_rows(elite_output, parent_index, child_count, tensor_count, gather_rows):
    local_rows = elite_output.shape[1]
    every_group = lax.all_gather(elite_output, "tensor", axis=2, tiled=True)
    span = child_count // tensor_count
    piece = local_rows // tensor_count
    pairs = []
    for source_child in range(child_count):
        for part in range(tensor_count):
            target_child = tensor_count * (source_child % span) + part
            target_tensor = source_child // span
            pairs.append(
                (source_child * tensor_count + part, target_child * tensor_count + target_tensor)
            )
    tensor_rank = lax.axis_index("tensor")
    mine = lax.dynamic_slice_in_dim(every_group, tensor_rank * piece, piece, axis=1)
    shuffled = lax.ppermute(mine, ("child", "tensor"), pairs)
    if gather_rows:
        gathered = lax.all_gather(shuffled, "child", axis=1, tiled=True)
        parent = parent_index[lax.axis_index("child")]
        return lax.dynamic_index_in_dim(gathered, parent, 0, keepdims=False)
    chosen = jnp.take(shuffled, parent_index, axis=0)
    return lax.all_to_all(chosen, "child", split_axis=0, concat_axis=1, tiled=True)[0]


GATHER_OUTPUT_ROWS = False


def on_device(
    tokens, episode, parent_index, mutation_seed, elite_project, elite_output, elite_bias
):
    child_rank = lax.axis_index("child")
    tensor_rank = lax.axis_index("tensor")
    child_count = lax.axis_size("child")
    tensor_count = lax.axis_size("tensor")
    kv_local = elite_project.shape[2]
    width_in = elite_project.shape[3]
    width_out = elite_output.shape[3]
    count_rows = tokens.shape[0]
    group_ids = tensor_rank * kv_local + jnp.arange(kv_local, dtype=jnp.int32)
    scale_in = MUTATION / math.sqrt(D)
    scale_out = MUTATION / math.sqrt(KV_HEADS * GROUP * HEAD_DIM)
    out_base = D * KV_HEADS * width_in
    bias_base = out_base + D * KV_HEADS * width_out
    own_seed = mutation_seed[0]
    parent = parent_index[child_rank]
    gathered_in = lax.all_gather(elite_project, "child", axis=1, tiled=True)
    arrived_in = lax.dynamic_index_in_dim(gathered_in, parent, 0, keepdims=False)
    arrived_out = output_rows(
        elite_output, parent_index, child_count, tensor_count, GATHER_OUTPUT_ROWS
    )
    every_row = jnp.arange(D, dtype=jnp.int32)
    child_in = (
        arrived_in.astype(jnp.float32)
        + scale_in * gaussian(own_seed, counter_grid(every_row, group_ids, width_in, 0))
    ).astype(jnp.bfloat16)
    out_rows = arrived_out.shape[0]
    own_rows = tensor_rank * out_rows + jnp.arange(out_rows, dtype=jnp.int32)
    all_groups = jnp.arange(KV_HEADS, dtype=jnp.int32)
    child_out = (
        arrived_out.astype(jnp.float32)
        + scale_out * gaussian(own_seed, counter_grid(own_rows, all_groups, width_out, out_base))
    ).astype(jnp.bfloat16)
    counter_bias = (
        bias_base + group_ids[:, None] * width_in + jnp.arange(width_in, dtype=jnp.int32)[None, :]
    )
    child_bias = elite_bias[parent] + BIAS_MUTATION * gaussian(own_seed, counter_bias)
    projected = (
        jnp.einsum("rd,dgc->rgc", tokens, child_in, preferred_element_type=jnp.float32)
        + child_bias[None]
    )
    allowed, cosine, sine_table = episode_tables(episode[0])
    query_part = projected[:, :, : GROUP * HEAD_DIM].reshape(count_rows, kv_local, GROUP, HEAD_DIM)
    key_part = projected[:, :, GROUP * HEAD_DIM : (GROUP + 1) * HEAD_DIM]
    value_part = projected[:, :, (GROUP + 1) * HEAD_DIM :]
    queries = rotary(query_part, cosine[:, None, None, :], sine_table[:, None, None, :]).astype(
        jnp.bfloat16
    )
    key_rows = rotary(key_part, cosine[:, None, :], sine_table[:, None, :]).astype(jnp.bfloat16)
    values = value_part.astype(jnp.bfloat16)
    scores = jnp.einsum("rgqh,sgh->gqrs", queries, key_rows, preferred_element_type=jnp.float32) * (
        1.0 / math.sqrt(HEAD_DIM)
    )
    masked = jnp.where(allowed[None, None], scores, -jnp.inf)
    row_max = jnp.max(masked, axis=-1, keepdims=True)
    weights = jnp.exp(masked - row_max)
    probability = (weights / jnp.sum(weights, axis=-1, keepdims=True)).astype(jnp.bfloat16)
    context = jnp.einsum(
        "gqrs,sgh->rgqh", probability, values, preferred_element_type=jnp.float32
    ).astype(jnp.bfloat16)
    context = context.reshape(count_rows, kv_local, width_out)
    every_context = lax.all_gather(context, "tensor", axis=1, tiled=True)
    attended = jnp.einsum(
        "rgc,dgc->rd", every_context, child_out, preferred_element_type=jnp.float32
    )
    return attended.astype(jnp.bfloat16)


def solution(mesh):
    in_specs = (
        P("child", None),
        P("child", None),
        P(),
        P("child"),
        P(None, "child", "tensor", None),
        P(None, "child", "tensor", None),
        P(None, "tensor", None),
    )
    out_specs = P("child", "tensor")
    return jax.shard_map(
        on_device, mesh=mesh, in_specs=in_specs, out_specs=out_specs, check_vma=False
    )
```

```python
import math

import jax
import jax.numpy as jnp
from jax import lax
from jax.sharding import PartitionSpec as P

D = 5120
HEAD_DIM = 128
KV_HEADS = 4
GROUP = 5


MUTATION = 0.25
BIAS_MUTATION = 0.05
ROPE_BASE = 1000000.0
NOISE_SPREAD = 147.80054


def mix_hash(seed_value, counter):
    hashed = counter + seed_value * jnp.int32(-1640531535)
    hashed = hashed ^ lax.shift_right_logical(hashed, jnp.full_like(hashed, 16))
    hashed = hashed * jnp.int32(-2048144789)
    hashed = hashed ^ lax.shift_right_logical(hashed, jnp.full_like(hashed, 13))
    hashed = hashed * jnp.int32(-1028477387)
    return hashed ^ lax.shift_right_logical(hashed, jnp.full_like(hashed, 16))


def gaussian(seed_value, counter):
    hashed = mix_hash(seed_value, counter)
    summed = jnp.bitwise_and(hashed, 255)
    summed = summed + jnp.bitwise_and(
        lax.shift_right_logical(hashed, jnp.full_like(hashed, 8)), 255
    )
    summed = summed + jnp.bitwise_and(
        lax.shift_right_logical(hashed, jnp.full_like(hashed, 16)), 255
    )
    summed = summed + lax.shift_right_logical(hashed, jnp.full_like(hashed, 24))
    return (summed - 510).astype(jnp.float32) / NOISE_SPREAD


def counter_grid(row_ids, group_ids, width, base):
    column_ids = jnp.arange(width, dtype=jnp.int32)
    return (
        base
        + (row_ids[:, None, None] * KV_HEADS + group_ids[None, :, None]) * width
        + column_ids[None, None, :]
    )


def rotary(vectors, cosine, sine_table):
    half_dim = vectors.shape[-1] // 2
    first_half = vectors[..., :half_dim]
    second_half = vectors[..., half_dim:]
    return jnp.concatenate(
        [
            first_half * cosine - second_half * sine_table,
            second_half * cosine + first_half * sine_table,
        ],
        axis=-1,
    )


def episode_tables(episode_row):
    count_rows = episode_row.shape[0]
    same_episode = episode_row[:, None] == episode_row[None, :]
    earlier = jnp.sum((episode_row[None, :] < episode_row[:, None]).astype(jnp.int32), axis=1)
    position = jnp.arange(count_rows, dtype=jnp.int32) - earlier
    causal = jnp.arange(count_rows)[None, :] <= jnp.arange(count_rows)[:, None]
    allowed = same_episode & causal
    frequency = jnp.exp(
        jnp.arange(0, HEAD_DIM, 2).astype(jnp.float32) * (-math.log(ROPE_BASE) / HEAD_DIM)
    )
    angles = position.astype(jnp.float32)[:, None] * frequency[None, :]
    return (allowed, jnp.cos(angles), jnp.sin(angles))


def output_rows(elite_output, parent_index, child_count, tensor_count, gather_rows):
    local_rows = elite_output.shape[1]
    every_group = lax.all_gather(elite_output, "tensor", axis=2, tiled=True)
    span = child_count // tensor_count
    piece = local_rows // tensor_count
    pairs = []
    for source_child in range(child_count):
        for part in range(tensor_count):
            target_child = tensor_count * (source_child % span) + part
            target_tensor = source_child // span
            pairs.append(
                (source_child * tensor_count + part, target_child * tensor_count + target_tensor)
            )
    tensor_rank = lax.axis_index("tensor")
    mine = lax.dynamic_slice_in_dim(every_group, tensor_rank * piece, piece, axis=1)
    shuffled = lax.ppermute(mine, ("child", "tensor"), pairs)
    if gather_rows:
        gathered = lax.all_gather(shuffled, "child", axis=1, tiled=True)
        parent = parent_index[lax.axis_index("child")]
        return lax.dynamic_index_in_dim(gathered, parent, 0, keepdims=False)
    chosen = jnp.take(shuffled, parent_index, axis=0)
    return lax.all_to_all(chosen, "child", split_axis=0, concat_axis=1, tiled=True)[0]


GATHER_OUTPUT_ROWS = True


def on_device(
    tokens, episode, parent_index, mutation_seed, elite_project, elite_output, elite_bias
):
    child_rank = lax.axis_index("child")
    tensor_rank = lax.axis_index("tensor")
    child_count = lax.axis_size("child")
    tensor_count = lax.axis_size("tensor")
    kv_local = elite_project.shape[2]
    width_in = elite_project.shape[3]
    width_out = elite_output.shape[3]
    count_rows = tokens.shape[0]
    group_ids = tensor_rank * kv_local + jnp.arange(kv_local, dtype=jnp.int32)
    scale_in = MUTATION / math.sqrt(D)
    scale_out = MUTATION / math.sqrt(KV_HEADS * GROUP * HEAD_DIM)
    out_base = D * KV_HEADS * width_in
    bias_base = out_base + D * KV_HEADS * width_out
    own_seed = mutation_seed[0]
    parent = parent_index[child_rank]
    gathered_in = lax.all_gather(elite_project, "child", axis=1, tiled=True)
    arrived_in = lax.dynamic_index_in_dim(gathered_in, parent, 0, keepdims=False)
    arrived_out = output_rows(
        elite_output, parent_index, child_count, tensor_count, GATHER_OUTPUT_ROWS
    )
    every_row = jnp.arange(D, dtype=jnp.int32)
    child_in = (
        arrived_in.astype(jnp.float32)
        + scale_in * gaussian(own_seed, counter_grid(every_row, group_ids, width_in, 0))
    ).astype(jnp.bfloat16)
    out_rows = arrived_out.shape[0]
    own_rows = tensor_rank * out_rows + jnp.arange(out_rows, dtype=jnp.int32)
    all_groups = jnp.arange(KV_HEADS, dtype=jnp.int32)
    child_out = (
        arrived_out.astype(jnp.float32)
        + scale_out * gaussian(own_seed, counter_grid(own_rows, all_groups, width_out, out_base))
    ).astype(jnp.bfloat16)
    counter_bias = (
        bias_base + group_ids[:, None] * width_in + jnp.arange(width_in, dtype=jnp.int32)[None, :]
    )
    child_bias = elite_bias[parent] + BIAS_MUTATION * gaussian(own_seed, counter_bias)
    projected = (
        jnp.einsum("rd,dgc->rgc", tokens, child_in, preferred_element_type=jnp.float32)
        + child_bias[None]
    )
    allowed, cosine, sine_table = episode_tables(episode[0])
    query_part = projected[:, :, : GROUP * HEAD_DIM].reshape(count_rows, kv_local, GROUP, HEAD_DIM)
    key_part = projected[:, :, GROUP * HEAD_DIM : (GROUP + 1) * HEAD_DIM]
    value_part = projected[:, :, (GROUP + 1) * HEAD_DIM :]
    queries = rotary(query_part, cosine[:, None, None, :], sine_table[:, None, None, :]).astype(
        jnp.bfloat16
    )
    key_rows = rotary(key_part, cosine[:, None, :], sine_table[:, None, :]).astype(jnp.bfloat16)
    values = value_part.astype(jnp.bfloat16)
    scores = jnp.einsum("rgqh,sgh->gqrs", queries, key_rows, preferred_element_type=jnp.float32) * (
        1.0 / math.sqrt(HEAD_DIM)
    )
    masked = jnp.where(allowed[None, None], scores, -jnp.inf)
    row_max = jnp.max(masked, axis=-1, keepdims=True)
    weights = jnp.exp(masked - row_max)
    probability = (weights / jnp.sum(weights, axis=-1, keepdims=True)).astype(jnp.bfloat16)
    context = jnp.einsum(
        "gqrs,sgh->rgqh", probability, values, preferred_element_type=jnp.float32
    ).astype(jnp.bfloat16)
    context = context.reshape(count_rows, kv_local, width_out)
    every_context = lax.all_gather(context, "tensor", axis=1, tiled=True)
    attended = jnp.einsum(
        "rgc,dgc->rd", every_context, child_out, preferred_element_type=jnp.float32
    )
    return attended.astype(jnp.bfloat16)


def solution(mesh):
    in_specs = (
        P("child", None),
        P("child", None),
        P(),
        P("child"),
        P(None, "child", "tensor", None),
        P(None, "child", "tensor", None),
        P(None, "tensor", None),
    )
    out_specs = P("child", "tensor")
    return jax.shard_map(
        on_device, mesh=mesh, in_specs=in_specs, out_specs=out_specs, check_vma=False
    )
```

```python
import math

import jax
import jax.numpy as jnp
from jax import lax
from jax.sharding import PartitionSpec as P

D = 5120
HEAD_DIM = 128
KV_HEADS = 4
GROUP = 5


MUTATION = 0.25
BIAS_MUTATION = 0.05
ROPE_BASE = 1000000.0
NOISE_SPREAD = 147.80054


def mix_hash(seed_value, counter):
    hashed = counter + seed_value * jnp.int32(-1640531535)
    hashed = hashed ^ lax.shift_right_logical(hashed, jnp.full_like(hashed, 16))
    hashed = hashed * jnp.int32(-2048144789)
    hashed = hashed ^ lax.shift_right_logical(hashed, jnp.full_like(hashed, 13))
    hashed = hashed * jnp.int32(-1028477387)
    return hashed ^ lax.shift_right_logical(hashed, jnp.full_like(hashed, 16))


def gaussian(seed_value, counter):
    hashed = mix_hash(seed_value, counter)
    summed = jnp.bitwise_and(hashed, 255)
    summed = summed + jnp.bitwise_and(
        lax.shift_right_logical(hashed, jnp.full_like(hashed, 8)), 255
    )
    summed = summed + jnp.bitwise_and(
        lax.shift_right_logical(hashed, jnp.full_like(hashed, 16)), 255
    )
    summed = summed + lax.shift_right_logical(hashed, jnp.full_like(hashed, 24))
    return (summed - 510).astype(jnp.float32) / NOISE_SPREAD


def counter_grid(row_ids, group_ids, width, base):
    column_ids = jnp.arange(width, dtype=jnp.int32)
    return (
        base
        + (row_ids[:, None, None] * KV_HEADS + group_ids[None, :, None]) * width
        + column_ids[None, None, :]
    )


def rotary(vectors, cosine, sine_table):
    half_dim = vectors.shape[-1] // 2
    first_half = vectors[..., :half_dim]
    second_half = vectors[..., half_dim:]
    return jnp.concatenate(
        [
            first_half * cosine - second_half * sine_table,
            second_half * cosine + first_half * sine_table,
        ],
        axis=-1,
    )


def episode_tables(episode_row):
    count_rows = episode_row.shape[0]
    same_episode = episode_row[:, None] == episode_row[None, :]
    earlier = jnp.sum((episode_row[None, :] < episode_row[:, None]).astype(jnp.int32), axis=1)
    position = jnp.arange(count_rows, dtype=jnp.int32) - earlier
    causal = jnp.arange(count_rows)[None, :] <= jnp.arange(count_rows)[:, None]
    allowed = same_episode & causal
    frequency = jnp.exp(
        jnp.arange(0, HEAD_DIM, 2).astype(jnp.float32) * (-math.log(ROPE_BASE) / HEAD_DIM)
    )
    angles = position.astype(jnp.float32)[:, None] * frequency[None, :]
    return (allowed, jnp.cos(angles), jnp.sin(angles))


CHILD = ("cx", "cz", "cy")


def ring_gather(block, axis_name, size):
    forward = [(j, (j + 1) % size) for j in range(size)]
    backward = [(j, (j - 1) % size) for j in range(size)]
    from_prev = lax.ppermute(block, axis_name, forward)
    from_next = lax.ppermute(block, axis_name, backward)
    half = block.shape[0] // 2
    far_low = lax.ppermute(from_prev[:half], axis_name, forward)
    far_high = lax.ppermute(from_next[half:], axis_name, backward)
    far = jnp.concatenate([far_low, far_high], axis=0)
    return jnp.stack([block, from_next, far, from_prev])


def shuffle_output_rows(elite_output, child_count, tensor_count):
    local_rows = elite_output.shape[1]
    every_group = lax.all_gather(elite_output, "tensor", axis=2, tiled=True)
    span = child_count // tensor_count
    piece = local_rows // tensor_count
    pairs = []
    for source_child in range(child_count):
        for part in range(tensor_count):
            target_child = tensor_count * (source_child % span) + part
            target_tensor = source_child // span
            pairs.append(
                (source_child * tensor_count + part, target_child * tensor_count + target_tensor)
            )
    tensor_rank = lax.axis_index("tensor")
    mine = lax.dynamic_slice_in_dim(every_group, tensor_rank * piece, piece, axis=1)
    return lax.ppermute(mine, CHILD + ("tensor",), pairs)


def on_device(
    tokens, episode, parent_index, mutation_seed, elite_project, elite_output, elite_bias
):
    side = lax.axis_size("cx")
    cx, cz, cy = (lax.axis_index(name) for name in CHILD)
    child_rank = lax.axis_index(CHILD)
    tensor_rank = lax.axis_index("tensor")
    child_count = lax.axis_size(CHILD)
    tensor_count = lax.axis_size("tensor")
    kv_local = elite_project.shape[2]
    width_in = elite_project.shape[3]
    width_out = elite_output.shape[3]
    count_rows = tokens.shape[0]
    group_ids = tensor_rank * kv_local + jnp.arange(kv_local, dtype=jnp.int32)
    scale_in = MUTATION / math.sqrt(D)
    scale_out = MUTATION / math.sqrt(KV_HEADS * GROUP * HEAD_DIM)
    out_base = D * KV_HEADS * width_in
    bias_base = out_base + D * KV_HEADS * width_out
    own_seed = mutation_seed[0]
    parent = parent_index[child_rank]
    gathered_in = lax.all_gather(elite_project, CHILD, axis=1, tiled=True)
    arrived_in = lax.dynamic_index_in_dim(gathered_in, parent, 0, keepdims=False)

    shuffled = shuffle_output_rows(elite_output, child_count, tensor_count)
    stage = ring_gather(shuffled, "cz", side)
    stage = ring_gather(stage, "cx", side)
    stage = ring_gather(stage, "cy", side)
    picked = lax.dynamic_index_in_dim(stage, parent, 3, keepdims=False)
    piece = picked.shape[3]
    arrived_out = picked.reshape(child_count * piece, KV_HEADS, width_out)
    offsets = jnp.arange(side, dtype=jnp.int32)
    source_child = (
        ((cx + offsets[None, :, None]) % side) * (side * side)
        + ((cz + offsets[None, None, :]) % side) * side
        + (cy + offsets[:, None, None]) % side
    ).reshape(child_count)
    out_rows = child_count * piece
    own_rows = tensor_rank * out_rows + (
        source_child[:, None] * piece + jnp.arange(piece, dtype=jnp.int32)[None, :]
    ).reshape(out_rows)

    every_row = jnp.arange(D, dtype=jnp.int32)
    child_in = (
        arrived_in.astype(jnp.float32)
        + scale_in * gaussian(own_seed, counter_grid(every_row, group_ids, width_in, 0))
    ).astype(jnp.bfloat16)
    all_groups = jnp.arange(KV_HEADS, dtype=jnp.int32)
    child_out = (
        arrived_out.astype(jnp.float32)
        + scale_out * gaussian(own_seed, counter_grid(own_rows, all_groups, width_out, out_base))
    ).astype(jnp.bfloat16)
    counter_bias = (
        bias_base + group_ids[:, None] * width_in + jnp.arange(width_in, dtype=jnp.int32)[None, :]
    )
    child_bias = elite_bias[parent] + BIAS_MUTATION * gaussian(own_seed, counter_bias)
    projected = (
        jnp.einsum("rd,dgc->rgc", tokens, child_in, preferred_element_type=jnp.float32)
        + child_bias[None]
    )
    allowed, cosine, sine_table = episode_tables(episode[0])
    query_part = projected[:, :, : GROUP * HEAD_DIM].reshape(count_rows, kv_local, GROUP, HEAD_DIM)
    key_part = projected[:, :, GROUP * HEAD_DIM : (GROUP + 1) * HEAD_DIM]
    value_part = projected[:, :, (GROUP + 1) * HEAD_DIM :]
    queries = rotary(query_part, cosine[:, None, None, :], sine_table[:, None, None, :]).astype(
        jnp.bfloat16
    )
    key_rows = rotary(key_part, cosine[:, None, :], sine_table[:, None, :]).astype(jnp.bfloat16)
    values = value_part.astype(jnp.bfloat16)
    scores = jnp.einsum("rgqh,sgh->gqrs", queries, key_rows, preferred_element_type=jnp.float32) * (
        1.0 / math.sqrt(HEAD_DIM)
    )
    masked = jnp.where(allowed[None, None], scores, -jnp.inf)
    row_max = jnp.max(masked, axis=-1, keepdims=True)
    weights = jnp.exp(masked - row_max)
    probability = (weights / jnp.sum(weights, axis=-1, keepdims=True)).astype(jnp.bfloat16)
    context = jnp.einsum(
        "gqrs,sgh->rgqh", probability, values, preferred_element_type=jnp.float32
    ).astype(jnp.bfloat16)
    context = context.reshape(count_rows, width_out)
    around = ring_gather(context, "tensor", tensor_count)
    every_context = jnp.take(around, (all_groups - tensor_rank) % tensor_count, axis=0)
    shuffled_attended = jnp.einsum(
        "grc,dgc->rd", every_context, child_out, preferred_element_type=jnp.float32
    ).astype(jnp.bfloat16)
    cxs = jnp.arange(child_count, dtype=jnp.int32) // (side * side)
    czs = (jnp.arange(child_count, dtype=jnp.int32) // side) % side
    cys = jnp.arange(child_count, dtype=jnp.int32) % side
    block_of = (
        ((cys - cy) % side) * (side * side) + ((cxs - cx) % side) * side + (czs - cz) % side
    )
    blocks = shuffled_attended.reshape(count_rows, child_count, piece)
    return jnp.take(blocks, block_of, axis=1).reshape(count_rows, out_rows)


def solution(mesh):
    side = round(mesh.shape["child"] ** (1.0 / 3.0))
    fine = jax.sharding.Mesh(
        mesh.devices.reshape(side, side, side, mesh.shape["tensor"]), CHILD + ("tensor",)
    )
    in_specs = (
        P(CHILD, None),
        P(CHILD, None),
        P(),
        P(CHILD),
        P(None, CHILD, "tensor", None),
        P(None, CHILD, "tensor", None),
        P(None, "tensor", None),
    )
    out_specs = P(CHILD, "tensor")
    return jax.shard_map(
        on_device, mesh=fine, in_specs=in_specs, out_specs=out_specs, check_vma=False
    )
```

```python
import math

import jax
import jax.numpy as jnp
from jax import lax
from jax.sharding import PartitionSpec as P

D = 5120
HEAD_DIM = 128
KV_HEADS = 4
GROUP = 5


MUTATION = 0.25
BIAS_MUTATION = 0.05
ROPE_BASE = 1000000.0
NOISE_SPREAD = 147.80054


def mix_hash(seed_value, counter):
    hashed = counter + seed_value * jnp.int32(-1640531535)
    hashed = hashed ^ lax.shift_right_logical(hashed, jnp.full_like(hashed, 16))
    hashed = hashed * jnp.int32(-2048144789)
    hashed = hashed ^ lax.shift_right_logical(hashed, jnp.full_like(hashed, 13))
    hashed = hashed * jnp.int32(-1028477387)
    return hashed ^ lax.shift_right_logical(hashed, jnp.full_like(hashed, 16))


def gaussian(seed_value, counter):
    hashed = mix_hash(seed_value, counter)
    summed = jnp.bitwise_and(hashed, 255)
    summed = summed + jnp.bitwise_and(
        lax.shift_right_logical(hashed, jnp.full_like(hashed, 8)), 255
    )
    summed = summed + jnp.bitwise_and(
        lax.shift_right_logical(hashed, jnp.full_like(hashed, 16)), 255
    )
    summed = summed + lax.shift_right_logical(hashed, jnp.full_like(hashed, 24))
    return (summed - 510).astype(jnp.float32) / NOISE_SPREAD


def noise_level(seed_value, counter):
    hashed = mix_hash(seed_value, counter)
    summed = jnp.bitwise_and(hashed, 255)
    summed = summed + jnp.bitwise_and(
        lax.shift_right_logical(hashed, jnp.full_like(hashed, 8)), 255
    )
    summed = summed + jnp.bitwise_and(
        lax.shift_right_logical(hashed, jnp.full_like(hashed, 16)), 255
    )
    summed = summed + lax.shift_right_logical(hashed, jnp.full_like(hashed, 24))
    return (summed - 510).astype(jnp.int16)


def counter_grid(row_ids, group_ids, width, base):
    column_ids = jnp.arange(width, dtype=jnp.int32)
    return (
        base
        + (row_ids[:, None, None] * KV_HEADS + group_ids[None, :, None]) * width
        + column_ids[None, None, :]
    )


def rotary(vectors, cosine, sine_table):
    half_dim = vectors.shape[-1] // 2
    first_half = vectors[..., :half_dim]
    second_half = vectors[..., half_dim:]
    return jnp.concatenate(
        [
            first_half * cosine - second_half * sine_table,
            second_half * cosine + first_half * sine_table,
        ],
        axis=-1,
    )


def episode_tables(episode_row):
    count_rows = episode_row.shape[0]
    same_episode = episode_row[:, None] == episode_row[None, :]
    earlier = jnp.sum((episode_row[None, :] < episode_row[:, None]).astype(jnp.int32), axis=1)
    position = jnp.arange(count_rows, dtype=jnp.int32) - earlier
    causal = jnp.arange(count_rows)[None, :] <= jnp.arange(count_rows)[:, None]
    allowed = same_episode & causal
    frequency = jnp.exp(
        jnp.arange(0, HEAD_DIM, 2).astype(jnp.float32) * (-math.log(ROPE_BASE) / HEAD_DIM)
    )
    angles = position.astype(jnp.float32)[:, None] * frequency[None, :]
    return (allowed, jnp.cos(angles), jnp.sin(angles))


CHILD = ("cx", "cz", "cy")


def ring_gather(block, axis_name, size):
    forward = [(j, (j + 1) % size) for j in range(size)]
    backward = [(j, (j - 1) % size) for j in range(size)]
    from_prev = lax.ppermute(block, axis_name, forward)
    from_next = lax.ppermute(block, axis_name, backward)
    half = block.shape[0] // 2
    far_low = lax.ppermute(from_prev[:half], axis_name, forward)
    far_high = lax.ppermute(from_next[half:], axis_name, backward)
    far = jnp.concatenate([far_low, far_high], axis=0)
    return jnp.stack([block, from_next, far, from_prev])


def shuffle_output_rows(elite_output, child_count, tensor_count):
    local_rows = elite_output.shape[1]
    every_group = lax.all_gather(elite_output, "tensor", axis=2, tiled=True)
    span = child_count // tensor_count
    piece = local_rows // tensor_count
    pairs = []
    for source_child in range(child_count):
        for part in range(tensor_count):
            target_child = tensor_count * (source_child % span) + part
            target_tensor = source_child // span
            pairs.append(
                (source_child * tensor_count + part, target_child * tensor_count + target_tensor)
            )
    tensor_rank = lax.axis_index("tensor")
    mine = lax.dynamic_slice_in_dim(every_group, tensor_rank * piece, piece, axis=1)
    return lax.ppermute(mine, CHILD + ("tensor",), pairs)


def on_device(
    tokens, episode, parent_index, mutation_seed, elite_project, elite_output, elite_bias
):
    side = lax.axis_size("cx")
    cx, cz, cy = (lax.axis_index(name) for name in CHILD)
    child_rank = lax.axis_index(CHILD)
    tensor_rank = lax.axis_index("tensor")
    child_count = lax.axis_size(CHILD)
    tensor_count = lax.axis_size("tensor")
    kv_local = elite_project.shape[2]
    width_in = elite_project.shape[3]
    width_out = elite_output.shape[3]
    count_rows = tokens.shape[0]
    group_ids = tensor_rank * kv_local + jnp.arange(kv_local, dtype=jnp.int32)
    scale_in = MUTATION / math.sqrt(D)
    scale_out = MUTATION / math.sqrt(KV_HEADS * GROUP * HEAD_DIM)
    out_base = D * KV_HEADS * width_in
    bias_base = out_base + D * KV_HEADS * width_out
    own_seed = mutation_seed[0]
    parent = parent_index[child_rank]
    gathered_in = lax.all_gather(elite_project, CHILD, axis=1, tiled=True)
    arrived_in = lax.dynamic_index_in_dim(gathered_in, parent, 0, keepdims=False)

    shuffled = shuffle_output_rows(elite_output, child_count, tensor_count)
    stage = ring_gather(shuffled, "cz", side)
    stage = ring_gather(stage, "cx", side)
    stage = ring_gather(stage, "cy", side)
    picked = lax.dynamic_index_in_dim(stage, parent, 3, keepdims=False)
    piece = picked.shape[3]
    arrived_out = picked.reshape(child_count * piece, KV_HEADS, width_out)
    offsets = jnp.arange(side, dtype=jnp.int32)
    source_child = (
        ((cx + offsets[None, :, None]) % side) * (side * side)
        + ((cz + offsets[None, None, :]) % side) * side
        + (cy + offsets[:, None, None]) % side
    ).reshape(child_count)
    out_rows = child_count * piece
    own_rows = tensor_rank * out_rows + (
        source_child[:, None] * piece + jnp.arange(piece, dtype=jnp.int32)[None, :]
    ).reshape(out_rows)

    every_row = jnp.arange(D, dtype=jnp.int32)
    all_groups = jnp.arange(KV_HEADS, dtype=jnp.int32)
    level_in, level_out = lax.optimization_barrier(
        (
            noise_level(own_seed, counter_grid(every_row, group_ids, width_in, 0)),
            noise_level(own_seed, counter_grid(own_rows, all_groups, width_out, out_base)),
        )
    )
    child_in = (
        arrived_in.astype(jnp.float32)
        + scale_in * (level_in.astype(jnp.float32) / NOISE_SPREAD)
    ).astype(jnp.bfloat16)
    child_out = (
        arrived_out.astype(jnp.float32)
        + scale_out * (level_out.astype(jnp.float32) / NOISE_SPREAD)
    ).astype(jnp.bfloat16)
    counter_bias = (
        bias_base + group_ids[:, None] * width_in + jnp.arange(width_in, dtype=jnp.int32)[None, :]
    )
    child_bias = elite_bias[parent] + BIAS_MUTATION * gaussian(own_seed, counter_bias)
    projected = (
        jnp.einsum("rd,dgc->rgc", tokens, child_in, preferred_element_type=jnp.float32)
        + child_bias[None]
    )
    allowed, cosine, sine_table = episode_tables(episode[0])
    query_part = projected[:, :, : GROUP * HEAD_DIM].reshape(count_rows, kv_local, GROUP, HEAD_DIM)
    key_part = projected[:, :, GROUP * HEAD_DIM : (GROUP + 1) * HEAD_DIM]
    value_part = projected[:, :, (GROUP + 1) * HEAD_DIM :]
    queries = rotary(query_part, cosine[:, None, None, :], sine_table[:, None, None, :]).astype(
        jnp.bfloat16
    )
    key_rows = rotary(key_part, cosine[:, None, :], sine_table[:, None, :]).astype(jnp.bfloat16)
    values = value_part.astype(jnp.bfloat16)
    scores = jnp.einsum("rgqh,sgh->gqrs", queries, key_rows, preferred_element_type=jnp.float32) * (
        1.0 / math.sqrt(HEAD_DIM)
    )
    masked = jnp.where(allowed[None, None], scores, -jnp.inf)
    row_max = jnp.max(masked, axis=-1, keepdims=True)
    weights = jnp.exp(masked - row_max)
    probability = (weights / jnp.sum(weights, axis=-1, keepdims=True)).astype(jnp.bfloat16)
    context = jnp.einsum(
        "gqrs,sgh->rgqh", probability, values, preferred_element_type=jnp.float32
    ).astype(jnp.bfloat16)
    context = context.reshape(count_rows, width_out)
    around = ring_gather(context, "tensor", tensor_count)
    every_context = jnp.take(around, (all_groups - tensor_rank) % tensor_count, axis=0)
    shuffled_attended = jnp.einsum(
        "grc,dgc->rd", every_context, child_out, preferred_element_type=jnp.float32
    ).astype(jnp.bfloat16)
    cxs = jnp.arange(child_count, dtype=jnp.int32) // (side * side)
    czs = (jnp.arange(child_count, dtype=jnp.int32) // side) % side
    cys = jnp.arange(child_count, dtype=jnp.int32) % side
    block_of = (
        ((cys - cy) % side) * (side * side) + ((cxs - cx) % side) * side + (czs - cz) % side
    )
    blocks = shuffled_attended.reshape(count_rows, child_count, piece)
    return jnp.take(blocks, block_of, axis=1).reshape(count_rows, out_rows)


def solution(mesh):
    side = round(mesh.shape["child"] ** (1.0 / 3.0))
    fine = jax.sharding.Mesh(
        mesh.devices.reshape(side, side, side, mesh.shape["tensor"]), CHILD + ("tensor",)
    )
    in_specs = (
        P(CHILD, None),
        P(CHILD, None),
        P(),
        P(CHILD),
        P(None, CHILD, "tensor", None),
        P(None, CHILD, "tensor", None),
        P(None, "tensor", None),
    )
    out_specs = P(CHILD, "tensor")
    return jax.shard_map(
        on_device, mesh=fine, in_specs=in_specs, out_specs=out_specs, check_vma=False
    )
```

```python
import math

import jax
import jax.numpy as jnp
from jax import lax
from jax.sharding import PartitionSpec as P

D = 5120
HEAD_DIM = 128
KV_HEADS = 4
GROUP = 5


MUTATION = 0.25
BIAS_MUTATION = 0.05
ROPE_BASE = 1000000.0
NOISE_SPREAD = 147.80054


def mix_hash(seed_value, counter):
    hashed = counter + seed_value * jnp.int32(-1640531535)
    hashed = hashed ^ lax.shift_right_logical(hashed, jnp.full_like(hashed, 16))
    hashed = hashed * jnp.int32(-2048144789)
    hashed = hashed ^ lax.shift_right_logical(hashed, jnp.full_like(hashed, 13))
    hashed = hashed * jnp.int32(-1028477387)
    return hashed ^ lax.shift_right_logical(hashed, jnp.full_like(hashed, 16))


def gaussian(seed_value, counter):
    hashed = mix_hash(seed_value, counter)
    summed = jnp.bitwise_and(hashed, 255)
    summed = summed + jnp.bitwise_and(
        lax.shift_right_logical(hashed, jnp.full_like(hashed, 8)), 255
    )
    summed = summed + jnp.bitwise_and(
        lax.shift_right_logical(hashed, jnp.full_like(hashed, 16)), 255
    )
    summed = summed + lax.shift_right_logical(hashed, jnp.full_like(hashed, 24))
    return (summed - 510).astype(jnp.float32) / NOISE_SPREAD


def noise_level(seed_value, counter):
    hashed = mix_hash(seed_value, counter)
    summed = jnp.bitwise_and(hashed, 255)
    summed = summed + jnp.bitwise_and(
        lax.shift_right_logical(hashed, jnp.full_like(hashed, 8)), 255
    )
    summed = summed + jnp.bitwise_and(
        lax.shift_right_logical(hashed, jnp.full_like(hashed, 16)), 255
    )
    summed = summed + lax.shift_right_logical(hashed, jnp.full_like(hashed, 24))
    return (summed - 510).astype(jnp.int16)


def counter_grid(row_ids, group_ids, width, base):
    column_ids = jnp.arange(width, dtype=jnp.int32)
    return (
        base
        + (row_ids[:, None, None] * KV_HEADS + group_ids[None, :, None]) * width
        + column_ids[None, None, :]
    )


def rotary(vectors, cosine, sine_table):
    half_dim = vectors.shape[-1] // 2
    first_half = vectors[..., :half_dim]
    second_half = vectors[..., half_dim:]
    return jnp.concatenate(
        [
            first_half * cosine - second_half * sine_table,
            second_half * cosine + first_half * sine_table,
        ],
        axis=-1,
    )


def episode_tables(episode_row):
    count_rows = episode_row.shape[0]
    same_episode = episode_row[:, None] == episode_row[None, :]
    earlier = jnp.sum((episode_row[None, :] < episode_row[:, None]).astype(jnp.int32), axis=1)
    position = jnp.arange(count_rows, dtype=jnp.int32) - earlier
    causal = jnp.arange(count_rows)[None, :] <= jnp.arange(count_rows)[:, None]
    allowed = same_episode & causal
    frequency = jnp.exp(
        jnp.arange(0, HEAD_DIM, 2).astype(jnp.float32) * (-math.log(ROPE_BASE) / HEAD_DIM)
    )
    angles = position.astype(jnp.float32)[:, None] * frequency[None, :]
    return (allowed, jnp.cos(angles), jnp.sin(angles))


CHILD = ("cx", "cz", "cy")


def ring_gather(block, axis_name, size):
    forward = [(j, (j + 1) % size) for j in range(size)]
    backward = [(j, (j - 1) % size) for j in range(size)]
    from_prev = lax.ppermute(block, axis_name, forward)
    from_next = lax.ppermute(block, axis_name, backward)
    half = block.shape[0] // 2
    far_low = lax.ppermute(from_prev[:half], axis_name, forward)
    far_high = lax.ppermute(from_next[half:], axis_name, backward)
    far = jnp.concatenate([far_low, far_high], axis=0)
    return jnp.stack([block, from_next, far, from_prev])


def shuffle_output_rows(elite_output, child_count, tensor_count):
    local_rows = elite_output.shape[1]
    every_group = lax.all_gather(elite_output, "tensor", axis=2, tiled=True)
    span = child_count // tensor_count
    piece = local_rows // tensor_count
    pairs = []
    for source_child in range(child_count):
        for part in range(tensor_count):
            target_child = tensor_count * (source_child % span) + part
            target_tensor = source_child // span
            pairs.append(
                (source_child * tensor_count + part, target_child * tensor_count + target_tensor)
            )
    tensor_rank = lax.axis_index("tensor")
    mine = lax.dynamic_slice_in_dim(every_group, tensor_rank * piece, piece, axis=1)
    return lax.ppermute(mine, CHILD + ("tensor",), pairs)


def on_device(
    tokens, episode, parent_index, mutation_seed, elite_project, elite_output, elite_bias
):
    side = lax.axis_size("cx")
    cx, cz, cy = (lax.axis_index(name) for name in CHILD)
    child_rank = lax.axis_index(CHILD)
    tensor_rank = lax.axis_index("tensor")
    child_count = lax.axis_size(CHILD)
    tensor_count = lax.axis_size("tensor")
    kv_local = elite_project.shape[2]
    width_in = elite_project.shape[3]
    width_out = elite_output.shape[3]
    count_rows = tokens.shape[0]
    group_ids = tensor_rank * kv_local + jnp.arange(kv_local, dtype=jnp.int32)
    scale_in = MUTATION / math.sqrt(D)
    scale_out = MUTATION / math.sqrt(KV_HEADS * GROUP * HEAD_DIM)
    out_base = D * KV_HEADS * width_in
    bias_base = out_base + D * KV_HEADS * width_out
    own_seed = mutation_seed[0]
    parent = parent_index[child_rank]
    gathered_in = lax.all_gather(elite_project, CHILD, axis=1, tiled=True)
    arrived_in = lax.dynamic_index_in_dim(gathered_in, parent, 0, keepdims=False)

    shuffled = shuffle_output_rows(elite_output, child_count, tensor_count)
    stage = ring_gather(shuffled, "cz", side)
    stage = ring_gather(stage, "cx", side)
    stage = ring_gather(stage, "cy", side)
    piece = stage.shape[4]
    offsets = jnp.arange(side, dtype=jnp.int32)
    source_child = (
        ((cx + offsets[None, :, None]) % side) * (side * side)
        + ((cz + offsets[None, None, :]) % side) * side
        + (cy + offsets[:, None, None]) % side
    ).reshape(child_count)
    out_rows = child_count * piece
    own_rows = tensor_rank * out_rows + (
        source_child[:, None] * piece + jnp.arange(piece, dtype=jnp.int32)[None, :]
    ).reshape(out_rows)

    every_row = jnp.arange(D, dtype=jnp.int32)
    all_groups = jnp.arange(KV_HEADS, dtype=jnp.int32)
    stage, level_in, level_out = lax.optimization_barrier(
        (
            stage,
            noise_level(own_seed, counter_grid(every_row, group_ids, width_in, 0)),
            noise_level(own_seed, counter_grid(own_rows, all_groups, width_out, out_base)),
        )
    )
    picked = lax.dynamic_index_in_dim(stage, parent, 3, keepdims=False)
    arrived_out = picked.reshape(child_count * piece, KV_HEADS, width_out)
    child_in = (
        arrived_in.astype(jnp.float32)
        + scale_in * (level_in.astype(jnp.float32) / NOISE_SPREAD)
    ).astype(jnp.bfloat16)
    child_out = (
        arrived_out.astype(jnp.float32)
        + scale_out * (level_out.astype(jnp.float32) / NOISE_SPREAD)
    ).astype(jnp.bfloat16)
    counter_bias = (
        bias_base + group_ids[:, None] * width_in + jnp.arange(width_in, dtype=jnp.int32)[None, :]
    )
    child_bias = elite_bias[parent] + BIAS_MUTATION * gaussian(own_seed, counter_bias)
    projected = (
        jnp.einsum("rd,dgc->rgc", tokens, child_in, preferred_element_type=jnp.float32)
        + child_bias[None]
    )
    allowed, cosine, sine_table = episode_tables(episode[0])
    query_part = projected[:, :, : GROUP * HEAD_DIM].reshape(count_rows, kv_local, GROUP, HEAD_DIM)
    key_part = projected[:, :, GROUP * HEAD_DIM : (GROUP + 1) * HEAD_DIM]
    value_part = projected[:, :, (GROUP + 1) * HEAD_DIM :]
    queries = rotary(query_part, cosine[:, None, None, :], sine_table[:, None, None, :]).astype(
        jnp.bfloat16
    )
    key_rows = rotary(key_part, cosine[:, None, :], sine_table[:, None, :]).astype(jnp.bfloat16)
    values = value_part.astype(jnp.bfloat16)
    scores = jnp.einsum("rgqh,sgh->gqrs", queries, key_rows, preferred_element_type=jnp.float32) * (
        1.0 / math.sqrt(HEAD_DIM)
    )
    masked = jnp.where(allowed[None, None], scores, -jnp.inf)
    row_max = jnp.max(masked, axis=-1, keepdims=True)
    weights = jnp.exp(masked - row_max)
    probability = (weights / jnp.sum(weights, axis=-1, keepdims=True)).astype(jnp.bfloat16)
    context = jnp.einsum(
        "gqrs,sgh->rgqh", probability, values, preferred_element_type=jnp.float32
    ).astype(jnp.bfloat16)
    context = context.reshape(count_rows, width_out)
    around = ring_gather(context, "tensor", tensor_count)
    every_context = jnp.take(around, (all_groups - tensor_rank) % tensor_count, axis=0)
    shuffled_attended = jnp.einsum(
        "grc,dgc->rd", every_context, child_out, preferred_element_type=jnp.float32
    ).astype(jnp.bfloat16)
    cxs = jnp.arange(child_count, dtype=jnp.int32) // (side * side)
    czs = (jnp.arange(child_count, dtype=jnp.int32) // side) % side
    cys = jnp.arange(child_count, dtype=jnp.int32) % side
    block_of = (
        ((cys - cy) % side) * (side * side) + ((cxs - cx) % side) * side + (czs - cz) % side
    )
    blocks = shuffled_attended.reshape(count_rows, child_count, piece)
    return jnp.take(blocks, block_of, axis=1).reshape(count_rows, out_rows)


def solution(mesh):
    side = round(mesh.shape["child"] ** (1.0 / 3.0))
    fine = jax.sharding.Mesh(
        mesh.devices.reshape(side, side, side, mesh.shape["tensor"]), CHILD + ("tensor",)
    )
    in_specs = (
        P(CHILD, None),
        P(CHILD, None),
        P(),
        P(CHILD),
        P(None, CHILD, "tensor", None),
        P(None, CHILD, "tensor", None),
        P(None, "tensor", None),
    )
    out_specs = P(CHILD, "tensor")
    return jax.shard_map(
        on_device, mesh=fine, in_specs=in_specs, out_specs=out_specs, check_vma=False
    )
```

```python
import math

import jax
import jax.numpy as jnp
from jax import lax
from jax.sharding import PartitionSpec as P

D = 5120
HEAD_DIM = 128
KV_HEADS = 4
GROUP = 5


MUTATION = 0.25
BIAS_MUTATION = 0.05
ROPE_BASE = 1000000.0
NOISE_SPREAD = 147.80054


def mix_hash(seed_value, counter):
    hashed = counter + seed_value * jnp.int32(-1640531535)
    hashed = hashed ^ lax.shift_right_logical(hashed, jnp.full_like(hashed, 16))
    hashed = hashed * jnp.int32(-2048144789)
    hashed = hashed ^ lax.shift_right_logical(hashed, jnp.full_like(hashed, 13))
    hashed = hashed * jnp.int32(-1028477387)
    return hashed ^ lax.shift_right_logical(hashed, jnp.full_like(hashed, 16))


def gaussian(seed_value, counter):
    hashed = mix_hash(seed_value, counter)
    summed = jnp.bitwise_and(hashed, 255)
    summed = summed + jnp.bitwise_and(
        lax.shift_right_logical(hashed, jnp.full_like(hashed, 8)), 255
    )
    summed = summed + jnp.bitwise_and(
        lax.shift_right_logical(hashed, jnp.full_like(hashed, 16)), 255
    )
    summed = summed + lax.shift_right_logical(hashed, jnp.full_like(hashed, 24))
    return (summed - 510).astype(jnp.float32) / NOISE_SPREAD


def counter_grid(row_ids, group_ids, width, base):
    column_ids = jnp.arange(width, dtype=jnp.int32)
    return (
        base
        + (row_ids[:, None, None] * KV_HEADS + group_ids[None, :, None]) * width
        + column_ids[None, None, :]
    )


def rotary(vectors, cosine, sine_table):
    half_dim = vectors.shape[-1] // 2
    first_half = vectors[..., :half_dim]
    second_half = vectors[..., half_dim:]
    return jnp.concatenate(
        [
            first_half * cosine - second_half * sine_table,
            second_half * cosine + first_half * sine_table,
        ],
        axis=-1,
    )


def episode_tables(episode_row):
    count_rows = episode_row.shape[0]
    same_episode = episode_row[:, None] == episode_row[None, :]
    earlier = jnp.sum((episode_row[None, :] < episode_row[:, None]).astype(jnp.int32), axis=1)
    position = jnp.arange(count_rows, dtype=jnp.int32) - earlier
    causal = jnp.arange(count_rows)[None, :] <= jnp.arange(count_rows)[:, None]
    allowed = same_episode & causal
    frequency = jnp.exp(
        jnp.arange(0, HEAD_DIM, 2).astype(jnp.float32) * (-math.log(ROPE_BASE) / HEAD_DIM)
    )
    angles = position.astype(jnp.float32)[:, None] * frequency[None, :]
    return (allowed, jnp.cos(angles), jnp.sin(angles))


CHILD = ("cx", "cz", "cy")


def ring_gather(block, axis_name, size, hold=None):
    forward = [(j, (j + 1) % size) for j in range(size)]
    backward = [(j, (j - 1) % size) for j in range(size)]
    from_prev = lax.ppermute(block, axis_name, forward)
    from_next = lax.ppermute(block, axis_name, backward)
    if hold is not None:
        from_prev, from_next, hold = lax.optimization_barrier((from_prev, from_next, hold))
    half = block.shape[0] // 2
    far_low = lax.ppermute(from_prev[:half], axis_name, forward)
    far_high = lax.ppermute(from_next[half:], axis_name, backward)
    far = jnp.concatenate([far_low, far_high], axis=0)
    stacked = jnp.stack([block, from_next, far, from_prev])
    return stacked if hold is None else (stacked, hold)


def shuffle_output_rows(elite_output, child_count, tensor_count):
    local_rows = elite_output.shape[1]
    every_group = lax.all_gather(elite_output, "tensor", axis=2, tiled=True)
    span = child_count // tensor_count
    piece = local_rows // tensor_count
    pairs = []
    for source_child in range(child_count):
        for part in range(tensor_count):
            target_child = tensor_count * (source_child % span) + part
            target_tensor = source_child // span
            pairs.append(
                (source_child * tensor_count + part, target_child * tensor_count + target_tensor)
            )
    tensor_rank = lax.axis_index("tensor")
    mine = lax.dynamic_slice_in_dim(every_group, tensor_rank * piece, piece, axis=1)
    return lax.ppermute(mine, CHILD + ("tensor",), pairs)


def on_device(
    tokens, episode, parent_index, mutation_seed, elite_project, elite_output, elite_bias
):
    side = lax.axis_size("cx")
    cx, cz, cy = (lax.axis_index(name) for name in CHILD)
    child_rank = lax.axis_index(CHILD)
    tensor_rank = lax.axis_index("tensor")
    child_count = lax.axis_size(CHILD)
    tensor_count = lax.axis_size("tensor")
    kv_local = elite_project.shape[2]
    width_in = elite_project.shape[3]
    width_out = elite_output.shape[3]
    count_rows = tokens.shape[0]
    group_ids = tensor_rank * kv_local + jnp.arange(kv_local, dtype=jnp.int32)
    scale_in = MUTATION / math.sqrt(D)
    scale_out = MUTATION / math.sqrt(KV_HEADS * GROUP * HEAD_DIM)
    out_base = D * KV_HEADS * width_in
    bias_base = out_base + D * KV_HEADS * width_out
    own_seed = mutation_seed[0]
    parent = parent_index[child_rank]
    gathered_in = lax.all_gather(elite_project, CHILD, axis=1, tiled=True)
    arrived_in = lax.dynamic_index_in_dim(gathered_in, parent, 0, keepdims=False)

    shuffled = shuffle_output_rows(elite_output, child_count, tensor_count)
    stage = ring_gather(shuffled, "cz", side)
    stage = ring_gather(stage, "cx", side)
    last_stage_input = stage
    piece = stage.shape[3]
    offsets = jnp.arange(side, dtype=jnp.int32)
    source_child = (
        ((cx + offsets[None, :, None]) % side) * (side * side)
        + ((cz + offsets[None, None, :]) % side) * side
        + (cy + offsets[:, None, None]) % side
    ).reshape(child_count)
    out_rows = child_count * piece
    own_rows = tensor_rank * out_rows + (
        source_child[:, None] * piece + jnp.arange(piece, dtype=jnp.int32)[None, :]
    ).reshape(out_rows)

    every_row = jnp.arange(D, dtype=jnp.int32)
    child_in = (
        arrived_in.astype(jnp.float32)
        + scale_in * gaussian(own_seed, counter_grid(every_row, group_ids, width_in, 0))
    ).astype(jnp.bfloat16)
    all_groups = jnp.arange(KV_HEADS, dtype=jnp.int32)
    counter_bias = (
        bias_base + group_ids[:, None] * width_in + jnp.arange(width_in, dtype=jnp.int32)[None, :]
    )
    child_bias = elite_bias[parent] + BIAS_MUTATION * gaussian(own_seed, counter_bias)
    projected = (
        jnp.einsum("rd,dgc->rgc", tokens, child_in, preferred_element_type=jnp.float32)
        + child_bias[None]
    )
    stage, projected = ring_gather(last_stage_input, "cy", side, hold=projected)
    picked = lax.dynamic_index_in_dim(stage, parent, 3, keepdims=False)
    arrived_out = picked.reshape(child_count * piece, KV_HEADS, width_out)
    child_out = (
        arrived_out.astype(jnp.float32)
        + scale_out * gaussian(own_seed, counter_grid(own_rows, all_groups, width_out, out_base))
    ).astype(jnp.bfloat16)
    allowed, cosine, sine_table = episode_tables(episode[0])
    query_part = projected[:, :, : GROUP * HEAD_DIM].reshape(count_rows, kv_local, GROUP, HEAD_DIM)
    key_part = projected[:, :, GROUP * HEAD_DIM : (GROUP + 1) * HEAD_DIM]
    value_part = projected[:, :, (GROUP + 1) * HEAD_DIM :]
    queries = rotary(query_part, cosine[:, None, None, :], sine_table[:, None, None, :]).astype(
        jnp.bfloat16
    )
    key_rows = rotary(key_part, cosine[:, None, :], sine_table[:, None, :]).astype(jnp.bfloat16)
    values = value_part.astype(jnp.bfloat16)
    scores = jnp.einsum("rgqh,sgh->gqrs", queries, key_rows, preferred_element_type=jnp.float32) * (
        1.0 / math.sqrt(HEAD_DIM)
    )
    masked = jnp.where(allowed[None, None], scores, -jnp.inf)
    row_max = jnp.max(masked, axis=-1, keepdims=True)
    weights = jnp.exp(masked - row_max)
    probability = (weights / jnp.sum(weights, axis=-1, keepdims=True)).astype(jnp.bfloat16)
    context = jnp.einsum(
        "gqrs,sgh->rgqh", probability, values, preferred_element_type=jnp.float32
    ).astype(jnp.bfloat16)
    context = context.reshape(count_rows, width_out)
    around = ring_gather(context, "tensor", tensor_count)
    every_context = jnp.take(around, (all_groups - tensor_rank) % tensor_count, axis=0)
    shuffled_attended = jnp.einsum(
        "grc,dgc->rd", every_context, child_out, preferred_element_type=jnp.float32
    ).astype(jnp.bfloat16)
    cxs = jnp.arange(child_count, dtype=jnp.int32) // (side * side)
    czs = (jnp.arange(child_count, dtype=jnp.int32) // side) % side
    cys = jnp.arange(child_count, dtype=jnp.int32) % side
    block_of = (
        ((cys - cy) % side) * (side * side) + ((cxs - cx) % side) * side + (czs - cz) % side
    )
    blocks = shuffled_attended.reshape(count_rows, child_count, piece)
    return jnp.take(blocks, block_of, axis=1).reshape(count_rows, out_rows)


def solution(mesh):
    side = round(mesh.shape["child"] ** (1.0 / 3.0))
    fine = jax.sharding.Mesh(
        mesh.devices.reshape(side, side, side, mesh.shape["tensor"]), CHILD + ("tensor",)
    )
    in_specs = (
        P(CHILD, None),
        P(CHILD, None),
        P(),
        P(CHILD),
        P(None, CHILD, "tensor", None),
        P(None, CHILD, "tensor", None),
        P(None, "tensor", None),
    )
    out_specs = P(CHILD, "tensor")
    return jax.shard_map(
        on_device, mesh=fine, in_specs=in_specs, out_specs=out_specs, check_vma=False
    )
```

```python
import math

import jax
import jax.numpy as jnp
from jax import lax
from jax.sharding import PartitionSpec as P

D = 5120
HEAD_DIM = 128
KV_HEADS = 4
GROUP = 5


MUTATION = 0.25
BIAS_MUTATION = 0.05
ROPE_BASE = 1000000.0
NOISE_SPREAD = 147.80054


def mix_hash(seed_value, counter):
    hashed = counter + seed_value * jnp.int32(-1640531535)
    hashed = hashed ^ lax.shift_right_logical(hashed, jnp.full_like(hashed, 16))
    hashed = hashed * jnp.int32(-2048144789)
    hashed = hashed ^ lax.shift_right_logical(hashed, jnp.full_like(hashed, 13))
    hashed = hashed * jnp.int32(-1028477387)
    return hashed ^ lax.shift_right_logical(hashed, jnp.full_like(hashed, 16))


def gaussian(seed_value, counter):
    hashed = mix_hash(seed_value, counter)
    summed = jnp.bitwise_and(hashed, 255)
    summed = summed + jnp.bitwise_and(
        lax.shift_right_logical(hashed, jnp.full_like(hashed, 8)), 255
    )
    summed = summed + jnp.bitwise_and(
        lax.shift_right_logical(hashed, jnp.full_like(hashed, 16)), 255
    )
    summed = summed + lax.shift_right_logical(hashed, jnp.full_like(hashed, 24))
    return (summed - 510).astype(jnp.float32) / NOISE_SPREAD


def counter_grid(row_ids, group_ids, width, base):
    column_ids = jnp.arange(width, dtype=jnp.int32)
    return (
        base
        + (row_ids[:, None, None] * KV_HEADS + group_ids[None, :, None]) * width
        + column_ids[None, None, :]
    )


def rotary(vectors, cosine, sine_table):
    half_dim = vectors.shape[-1] // 2
    first_half = vectors[..., :half_dim]
    second_half = vectors[..., half_dim:]
    return jnp.concatenate(
        [
            first_half * cosine - second_half * sine_table,
            second_half * cosine + first_half * sine_table,
        ],
        axis=-1,
    )


def episode_tables(episode_row):
    count_rows = episode_row.shape[0]
    same_episode = episode_row[:, None] == episode_row[None, :]
    earlier = jnp.sum((episode_row[None, :] < episode_row[:, None]).astype(jnp.int32), axis=1)
    position = jnp.arange(count_rows, dtype=jnp.int32) - earlier
    causal = jnp.arange(count_rows)[None, :] <= jnp.arange(count_rows)[:, None]
    allowed = same_episode & causal
    frequency = jnp.exp(
        jnp.arange(0, HEAD_DIM, 2).astype(jnp.float32) * (-math.log(ROPE_BASE) / HEAD_DIM)
    )
    angles = position.astype(jnp.float32)[:, None] * frequency[None, :]
    return (allowed, jnp.cos(angles), jnp.sin(angles))


CHILD = ("cx", "cz", "cy")


def ring_gather(block, axis_name, size, hold=None):
    forward = [(j, (j + 1) % size) for j in range(size)]
    backward = [(j, (j - 1) % size) for j in range(size)]
    from_prev = lax.ppermute(block, axis_name, forward)
    from_next = lax.ppermute(block, axis_name, backward)
    if hold is not None:
        from_prev, from_next, hold = lax.optimization_barrier((from_prev, from_next, hold))
    half = block.shape[0] // 2
    far_low = lax.ppermute(from_prev[:half], axis_name, forward)
    far_high = lax.ppermute(from_next[half:], axis_name, backward)
    if hold is not None:
        pieces = [(0, 0, block), (1, 0, from_next), (2, 0, far_low), (2, half, far_high),
                  (3, 0, from_prev)]
        return pieces, hold
    far = jnp.concatenate([far_low, far_high], axis=0)
    return jnp.stack([block, from_next, far, from_prev])


def shuffle_output_rows(elite_output, child_count, tensor_count):
    local_rows = elite_output.shape[1]
    every_group = lax.all_gather(elite_output, "tensor", axis=2, tiled=True)
    span = child_count // tensor_count
    piece = local_rows // tensor_count
    pairs = []
    for source_child in range(child_count):
        for part in range(tensor_count):
            target_child = tensor_count * (source_child % span) + part
            target_tensor = source_child // span
            pairs.append(
                (source_child * tensor_count + part, target_child * tensor_count + target_tensor)
            )
    tensor_rank = lax.axis_index("tensor")
    mine = lax.dynamic_slice_in_dim(every_group, tensor_rank * piece, piece, axis=1)
    return lax.ppermute(mine, CHILD + ("tensor",), pairs)


def on_device(
    tokens, episode, parent_index, mutation_seed, elite_project, elite_output, elite_bias
):
    side = lax.axis_size("cx")
    cx, cz, cy = (lax.axis_index(name) for name in CHILD)
    child_rank = lax.axis_index(CHILD)
    tensor_rank = lax.axis_index("tensor")
    child_count = lax.axis_size(CHILD)
    tensor_count = lax.axis_size("tensor")
    kv_local = elite_project.shape[2]
    width_in = elite_project.shape[3]
    width_out = elite_output.shape[3]
    count_rows = tokens.shape[0]
    group_ids = tensor_rank * kv_local + jnp.arange(kv_local, dtype=jnp.int32)
    scale_in = MUTATION / math.sqrt(D)
    scale_out = MUTATION / math.sqrt(KV_HEADS * GROUP * HEAD_DIM)
    out_base = D * KV_HEADS * width_in
    bias_base = out_base + D * KV_HEADS * width_out
    own_seed = mutation_seed[0]
    parent = parent_index[child_rank]
    gathered_in = lax.all_gather(elite_project, CHILD, axis=1, tiled=True)
    arrived_in = lax.dynamic_index_in_dim(gathered_in, parent, 0, keepdims=False)

    shuffled = shuffle_output_rows(elite_output, child_count, tensor_count)
    stage = ring_gather(shuffled, "cz", side)
    stage = ring_gather(stage, "cx", side)
    last_stage_input = stage
    piece = stage.shape[3]
    offsets = jnp.arange(side, dtype=jnp.int32)
    out_rows = child_count * piece

    every_row = jnp.arange(D, dtype=jnp.int32)
    child_in = (
        arrived_in.astype(jnp.float32)
        + scale_in * gaussian(own_seed, counter_grid(every_row, group_ids, width_in, 0))
    ).astype(jnp.bfloat16)
    all_groups = jnp.arange(KV_HEADS, dtype=jnp.int32)
    counter_bias = (
        bias_base + group_ids[:, None] * width_in + jnp.arange(width_in, dtype=jnp.int32)[None, :]
    )
    child_bias = elite_bias[parent] + BIAS_MUTATION * gaussian(own_seed, counter_bias)
    projected = (
        jnp.einsum("rd,dgc->rgc", tokens, child_in, preferred_element_type=jnp.float32)
        + child_bias[None]
    )
    pieces, projected = ring_gather(last_stage_input, "cy", side, hold=projected)
    allowed, cosine, sine_table = episode_tables(episode[0])
    query_part = projected[:, :, : GROUP * HEAD_DIM].reshape(count_rows, kv_local, GROUP, HEAD_DIM)
    key_part = projected[:, :, GROUP * HEAD_DIM : (GROUP + 1) * HEAD_DIM]
    value_part = projected[:, :, (GROUP + 1) * HEAD_DIM :]
    queries = rotary(query_part, cosine[:, None, None, :], sine_table[:, None, None, :]).astype(
        jnp.bfloat16
    )
    key_rows = rotary(key_part, cosine[:, None, :], sine_table[:, None, :]).astype(jnp.bfloat16)
    values = value_part.astype(jnp.bfloat16)
    scores = jnp.einsum("rgqh,sgh->gqrs", queries, key_rows, preferred_element_type=jnp.float32) * (
        1.0 / math.sqrt(HEAD_DIM)
    )
    masked = jnp.where(allowed[None, None], scores, -jnp.inf)
    row_max = jnp.max(masked, axis=-1, keepdims=True)
    weights = jnp.exp(masked - row_max)
    probability = (weights / jnp.sum(weights, axis=-1, keepdims=True)).astype(jnp.bfloat16)
    context = jnp.einsum(
        "gqrs,sgh->rgqh", probability, values, preferred_element_type=jnp.float32
    ).astype(jnp.bfloat16)
    context = context.reshape(count_rows, width_out)
    around = ring_gather(context, "tensor", tensor_count)
    every_context = jnp.take(around, (all_groups - tensor_rank) % tensor_count, axis=0)
    parts = []
    for dy, first, part in pieces:
        picked = lax.dynamic_index_in_dim(part, parent, 2, keepdims=False)
        count_dx = picked.shape[0]
        part_child = (
            ((cx + first + jnp.arange(count_dx, dtype=jnp.int32)[:, None]) % side) * (side * side)
            + ((cz + offsets[None, :]) % side) * side
            + (cy + dy) % side
        ).reshape(-1)
        part_rows = tensor_rank * out_rows + (
            part_child[:, None] * piece + jnp.arange(piece, dtype=jnp.int32)[None, :]
        ).reshape(-1)
        part_out = (
            picked.reshape(-1, KV_HEADS, width_out).astype(jnp.float32)
            + scale_out
            * gaussian(own_seed, counter_grid(part_rows, all_groups, width_out, out_base))
        ).astype(jnp.bfloat16)
        parts.append(
            jnp.einsum(
                "grc,dgc->rd", every_context, part_out, preferred_element_type=jnp.float32
            ).astype(jnp.bfloat16)
        )
    shuffled_attended = jnp.concatenate(parts, axis=1)
    cxs = jnp.arange(child_count, dtype=jnp.int32) // (side * side)
    czs = (jnp.arange(child_count, dtype=jnp.int32) // side) % side
    cys = jnp.arange(child_count, dtype=jnp.int32) % side
    block_of = (
        ((cys - cy) % side) * (side * side) + ((cxs - cx) % side) * side + (czs - cz) % side
    )
    blocks = shuffled_attended.reshape(count_rows, child_count, piece)
    return jnp.take(blocks, block_of, axis=1).reshape(count_rows, out_rows)


def solution(mesh):
    side = round(mesh.shape["child"] ** (1.0 / 3.0))
    fine = jax.sharding.Mesh(
        mesh.devices.reshape(side, side, side, mesh.shape["tensor"]), CHILD + ("tensor",)
    )
    in_specs = (
        P(CHILD, None),
        P(CHILD, None),
        P(),
        P(CHILD),
        P(None, CHILD, "tensor", None),
        P(None, CHILD, "tensor", None),
        P(None, "tensor", None),
    )
    out_specs = P(CHILD, "tensor")
    return jax.shard_map(
        on_device, mesh=fine, in_specs=in_specs, out_specs=out_specs, check_vma=False
    )
```

```python
import math

import jax
import jax.numpy as jnp
from jax import lax
from jax.sharding import PartitionSpec as P

D = 5120
HEAD_DIM = 128
KV_HEADS = 4
GROUP = 5


MUTATION = 0.25
BIAS_MUTATION = 0.05
ROPE_BASE = 1000000.0
NOISE_SPREAD = 147.80054


def mix_hash(seed_value, counter):
    hashed = counter + seed_value * jnp.int32(-1640531535)
    hashed = hashed ^ lax.shift_right_logical(hashed, jnp.full_like(hashed, 16))
    hashed = hashed * jnp.int32(-2048144789)
    hashed = hashed ^ lax.shift_right_logical(hashed, jnp.full_like(hashed, 13))
    hashed = hashed * jnp.int32(-1028477387)
    return hashed ^ lax.shift_right_logical(hashed, jnp.full_like(hashed, 16))


def gaussian(seed_value, counter):
    hashed = mix_hash(seed_value, counter)
    summed = jnp.bitwise_and(hashed, 255)
    summed = summed + jnp.bitwise_and(
        lax.shift_right_logical(hashed, jnp.full_like(hashed, 8)), 255
    )
    summed = summed + jnp.bitwise_and(
        lax.shift_right_logical(hashed, jnp.full_like(hashed, 16)), 255
    )
    summed = summed + lax.shift_right_logical(hashed, jnp.full_like(hashed, 24))
    return (summed - 510).astype(jnp.float32) / NOISE_SPREAD


def counter_grid(row_ids, group_ids, width, base):
    column_ids = jnp.arange(width, dtype=jnp.int32)
    return (
        base
        + (row_ids[:, None, None] * KV_HEADS + group_ids[None, :, None]) * width
        + column_ids[None, None, :]
    )


def rotary(vectors, cosine, sine_table):
    half_dim = vectors.shape[-1] // 2
    first_half = vectors[..., :half_dim]
    second_half = vectors[..., half_dim:]
    return jnp.concatenate(
        [
            first_half * cosine - second_half * sine_table,
            second_half * cosine + first_half * sine_table,
        ],
        axis=-1,
    )


def episode_tables(episode_row):
    count_rows = episode_row.shape[0]
    same_episode = episode_row[:, None] == episode_row[None, :]
    earlier = jnp.sum((episode_row[None, :] < episode_row[:, None]).astype(jnp.int32), axis=1)
    position = jnp.arange(count_rows, dtype=jnp.int32) - earlier
    causal = jnp.arange(count_rows)[None, :] <= jnp.arange(count_rows)[:, None]
    allowed = same_episode & causal
    frequency = jnp.exp(
        jnp.arange(0, HEAD_DIM, 2).astype(jnp.float32) * (-math.log(ROPE_BASE) / HEAD_DIM)
    )
    angles = position.astype(jnp.float32)[:, None] * frequency[None, :]
    return (allowed, jnp.cos(angles), jnp.sin(angles))


CHILD = ("cx", "cz", "cy")


def ring_gather(block, axis_name, size, hold=None):
    forward = [(j, (j + 1) % size) for j in range(size)]
    backward = [(j, (j - 1) % size) for j in range(size)]
    from_prev = lax.ppermute(block, axis_name, forward)
    from_next = lax.ppermute(block, axis_name, backward)
    if hold is not None:
        from_prev, from_next, hold = lax.optimization_barrier((from_prev, from_next, hold))
    half = block.shape[0] // 2
    far_low = lax.ppermute(from_prev[:half], axis_name, forward)
    far_high = lax.ppermute(from_next[half:], axis_name, backward)
    if hold is not None:
        pieces = [(0, 0, block), (1, 0, from_next), (2, 0, far_low), (2, half, far_high),
                  (3, 0, from_prev)]
        return pieces, hold
    far = jnp.concatenate([far_low, far_high], axis=0)
    return jnp.stack([block, from_next, far, from_prev])


def shuffle_output_rows(elite_output, child_count, tensor_count):
    local_rows = elite_output.shape[1]
    every_group = lax.all_gather(elite_output, "tensor", axis=2, tiled=True)
    span = child_count // tensor_count
    piece = local_rows // tensor_count
    pairs = []
    for source_child in range(child_count):
        for part in range(tensor_count):
            target_child = tensor_count * (source_child % span) + part
            target_tensor = source_child // span
            pairs.append(
                (source_child * tensor_count + part, target_child * tensor_count + target_tensor)
            )
    tensor_rank = lax.axis_index("tensor")
    mine = lax.dynamic_slice_in_dim(every_group, tensor_rank * piece, piece, axis=1)
    return lax.ppermute(mine, CHILD + ("tensor",), pairs)


def on_device(
    tokens, episode, parent_index, mutation_seed, elite_project, elite_output, elite_bias
):
    side = lax.axis_size("cx")
    cx, cz, cy = (lax.axis_index(name) for name in CHILD)
    child_rank = lax.axis_index(CHILD)
    tensor_rank = lax.axis_index("tensor")
    child_count = lax.axis_size(CHILD)
    tensor_count = lax.axis_size("tensor")
    kv_local = elite_project.shape[2]
    width_in = elite_project.shape[3]
    width_out = elite_output.shape[3]
    count_rows = tokens.shape[0]
    group_ids = tensor_rank * kv_local + jnp.arange(kv_local, dtype=jnp.int32)
    scale_in = MUTATION / math.sqrt(D)
    scale_out = MUTATION / math.sqrt(KV_HEADS * GROUP * HEAD_DIM)
    out_base = D * KV_HEADS * width_in
    bias_base = out_base + D * KV_HEADS * width_out
    own_seed = mutation_seed[0]
    parent = parent_index[child_rank]
    local_in = elite_project.shape[1]
    split_in = local_in // 2
    halves_in = [
        lax.all_gather(elite_project[:, :split_in], CHILD, axis=1, tiled=False),
        lax.all_gather(elite_project[:, split_in:], CHILD, axis=1, tiled=False),
    ]

    shuffled = shuffle_output_rows(elite_output, child_count, tensor_count)
    stage = ring_gather(shuffled, "cz", side)
    stage = ring_gather(stage, "cx", side)
    last_stage_input = stage
    piece = stage.shape[3]
    offsets = jnp.arange(side, dtype=jnp.int32)
    out_rows = child_count * piece

    member_tokens = tokens.reshape(count_rows, child_count, local_in)
    projected = None
    for half, (first, gathered) in enumerate(zip((0, split_in), halves_in)):
        if projected is not None:
            gathered, projected = lax.optimization_barrier((gathered, projected))
        arrived = lax.dynamic_index_in_dim(gathered, parent, 0, keepdims=False)
        width_rows = arrived.shape[1]
        rows = (
            jnp.arange(child_count, dtype=jnp.int32)[:, None] * local_in
            + first
            + jnp.arange(width_rows, dtype=jnp.int32)[None, :]
        ).reshape(-1)
        child_half = (
            arrived.reshape(-1, kv_local, width_in).astype(jnp.float32)
            + scale_in * gaussian(own_seed, counter_grid(rows, group_ids, width_in, 0))
        ).astype(jnp.bfloat16)
        token_half = member_tokens[:, :, first : first + width_rows].reshape(count_rows, -1)
        part = jnp.einsum(
            "rd,dgc->rgc", token_half, child_half, preferred_element_type=jnp.float32
        )
        projected = part if projected is None else projected + part
    all_groups = jnp.arange(KV_HEADS, dtype=jnp.int32)
    counter_bias = (
        bias_base + group_ids[:, None] * width_in + jnp.arange(width_in, dtype=jnp.int32)[None, :]
    )
    child_bias = elite_bias[parent] + BIAS_MUTATION * gaussian(own_seed, counter_bias)
    projected = projected + child_bias[None]
    pieces, projected = ring_gather(last_stage_input, "cy", side, hold=projected)
    allowed, cosine, sine_table = episode_tables(episode[0])
    query_part = projected[:, :, : GROUP * HEAD_DIM].reshape(count_rows, kv_local, GROUP, HEAD_DIM)
    key_part = projected[:, :, GROUP * HEAD_DIM : (GROUP + 1) * HEAD_DIM]
    value_part = projected[:, :, (GROUP + 1) * HEAD_DIM :]
    queries = rotary(query_part, cosine[:, None, None, :], sine_table[:, None, None, :]).astype(
        jnp.bfloat16
    )
    key_rows = rotary(key_part, cosine[:, None, :], sine_table[:, None, :]).astype(jnp.bfloat16)
    values = value_part.astype(jnp.bfloat16)
    scores = jnp.einsum("rgqh,sgh->gqrs", queries, key_rows, preferred_element_type=jnp.float32) * (
        1.0 / math.sqrt(HEAD_DIM)
    )
    masked = jnp.where(allowed[None, None], scores, -jnp.inf)
    row_max = jnp.max(masked, axis=-1, keepdims=True)
    weights = jnp.exp(masked - row_max)
    probability = (weights / jnp.sum(weights, axis=-1, keepdims=True)).astype(jnp.bfloat16)
    context = jnp.einsum(
        "gqrs,sgh->rgqh", probability, values, preferred_element_type=jnp.float32
    ).astype(jnp.bfloat16)
    context = context.reshape(count_rows, width_out)
    around = ring_gather(context, "tensor", tensor_count)
    every_context = jnp.take(around, (all_groups - tensor_rank) % tensor_count, axis=0)
    parts = []
    for dy, first, part in pieces:
        picked = lax.dynamic_index_in_dim(part, parent, 2, keepdims=False)
        count_dx = picked.shape[0]
        part_child = (
            ((cx + first + jnp.arange(count_dx, dtype=jnp.int32)[:, None]) % side) * (side * side)
            + ((cz + offsets[None, :]) % side) * side
            + (cy + dy) % side
        ).reshape(-1)
        part_rows = tensor_rank * out_rows + (
            part_child[:, None] * piece + jnp.arange(piece, dtype=jnp.int32)[None, :]
        ).reshape(-1)
        part_out = (
            picked.reshape(-1, KV_HEADS, width_out).astype(jnp.float32)
            + scale_out
            * gaussian(own_seed, counter_grid(part_rows, all_groups, width_out, out_base))
        ).astype(jnp.bfloat16)
        parts.append(
            jnp.einsum(
                "grc,dgc->rd", every_context, part_out, preferred_element_type=jnp.float32
            ).astype(jnp.bfloat16)
        )
    shuffled_attended = jnp.concatenate(parts, axis=1)
    cxs = jnp.arange(child_count, dtype=jnp.int32) // (side * side)
    czs = (jnp.arange(child_count, dtype=jnp.int32) // side) % side
    cys = jnp.arange(child_count, dtype=jnp.int32) % side
    block_of = (
        ((cys - cy) % side) * (side * side) + ((cxs - cx) % side) * side + (czs - cz) % side
    )
    blocks = shuffled_attended.reshape(count_rows, child_count, piece)
    return jnp.take(blocks, block_of, axis=1).reshape(count_rows, out_rows)


def solution(mesh):
    side = round(mesh.shape["child"] ** (1.0 / 3.0))
    fine = jax.sharding.Mesh(
        mesh.devices.reshape(side, side, side, mesh.shape["tensor"]), CHILD + ("tensor",)
    )
    in_specs = (
        P(CHILD, None),
        P(CHILD, None),
        P(),
        P(CHILD),
        P(None, CHILD, "tensor", None),
        P(None, CHILD, "tensor", None),
        P(None, "tensor", None),
    )
    out_specs = P(CHILD, "tensor")
    return jax.shard_map(
        on_device, mesh=fine, in_specs=in_specs, out_specs=out_specs, check_vma=False
    )
```

```python
import math

import jax
import jax.numpy as jnp
from jax import lax
from jax.sharding import PartitionSpec as P

D = 5120
HEAD_DIM = 128
KV_HEADS = 4
GROUP = 5


MUTATION = 0.25
BIAS_MUTATION = 0.05
ROPE_BASE = 1000000.0
NOISE_SPREAD = 147.80054


def mix_hash(seed_value, counter):
    hashed = counter + seed_value * jnp.int32(-1640531535)
    hashed = hashed ^ lax.shift_right_logical(hashed, jnp.full_like(hashed, 16))
    hashed = hashed * jnp.int32(-2048144789)
    hashed = hashed ^ lax.shift_right_logical(hashed, jnp.full_like(hashed, 13))
    hashed = hashed * jnp.int32(-1028477387)
    return hashed ^ lax.shift_right_logical(hashed, jnp.full_like(hashed, 16))


def gaussian(seed_value, counter):
    hashed = mix_hash(seed_value, counter)
    summed = jnp.bitwise_and(hashed, 255)
    summed = summed + jnp.bitwise_and(
        lax.shift_right_logical(hashed, jnp.full_like(hashed, 8)), 255
    )
    summed = summed + jnp.bitwise_and(
        lax.shift_right_logical(hashed, jnp.full_like(hashed, 16)), 255
    )
    summed = summed + lax.shift_right_logical(hashed, jnp.full_like(hashed, 24))
    return (summed - 510).astype(jnp.float32) / NOISE_SPREAD


def counter_grid(row_ids, group_ids, width, base):
    column_ids = jnp.arange(width, dtype=jnp.int32)
    return (
        base
        + (row_ids[:, None, None] * KV_HEADS + group_ids[None, :, None]) * width
        + column_ids[None, None, :]
    )


def rotary(vectors, cosine, sine_table):
    half_dim = vectors.shape[-1] // 2
    first_half = vectors[..., :half_dim]
    second_half = vectors[..., half_dim:]
    return jnp.concatenate(
        [
            first_half * cosine - second_half * sine_table,
            second_half * cosine + first_half * sine_table,
        ],
        axis=-1,
    )


def episode_tables(episode_row):
    count_rows = episode_row.shape[0]
    same_episode = episode_row[:, None] == episode_row[None, :]
    earlier = jnp.sum((episode_row[None, :] < episode_row[:, None]).astype(jnp.int32), axis=1)
    position = jnp.arange(count_rows, dtype=jnp.int32) - earlier
    causal = jnp.arange(count_rows)[None, :] <= jnp.arange(count_rows)[:, None]
    allowed = same_episode & causal
    frequency = jnp.exp(
        jnp.arange(0, HEAD_DIM, 2).astype(jnp.float32) * (-math.log(ROPE_BASE) / HEAD_DIM)
    )
    angles = position.astype(jnp.float32)[:, None] * frequency[None, :]
    return (allowed, jnp.cos(angles), jnp.sin(angles))


CHILD = ("cx", "cz", "cy")


def ring_gather(block, axis_name, size, hold=None):
    forward = [(j, (j + 1) % size) for j in range(size)]
    backward = [(j, (j - 1) % size) for j in range(size)]
    from_prev = lax.ppermute(block, axis_name, forward)
    from_next = lax.ppermute(block, axis_name, backward)
    if hold is not None:
        from_prev, from_next, hold = lax.optimization_barrier((from_prev, from_next, hold))
    half = block.shape[0] // 2
    far_low = lax.ppermute(from_prev[:half], axis_name, forward)
    far_high = lax.ppermute(from_next[half:], axis_name, backward)
    if hold is not None:
        pieces = [(0, 0, block), (1, 0, from_next), (2, 0, far_low), (2, half, far_high),
                  (3, 0, from_prev)]
        return pieces, hold
    far = jnp.concatenate([far_low, far_high], axis=0)
    return jnp.stack([block, from_next, far, from_prev])


def shuffle_output_rows(elite_output, child_count, tensor_count):
    local_rows = elite_output.shape[1]
    every_group = lax.all_gather(elite_output, "tensor", axis=2, tiled=True)
    span = child_count // tensor_count
    piece = local_rows // tensor_count
    pairs = []
    for source_child in range(child_count):
        for part in range(tensor_count):
            target_child = tensor_count * (source_child % span) + part
            target_tensor = source_child // span
            pairs.append(
                (source_child * tensor_count + part, target_child * tensor_count + target_tensor)
            )
    tensor_rank = lax.axis_index("tensor")
    mine = lax.dynamic_slice_in_dim(every_group, tensor_rank * piece, piece, axis=1)
    return lax.ppermute(mine, CHILD + ("tensor",), pairs)


def on_device(
    tokens, episode, parent_index, mutation_seed, elite_project, elite_output, elite_bias
):
    side = lax.axis_size("cx")
    cx, cz, cy = (lax.axis_index(name) for name in CHILD)
    child_rank = lax.axis_index(CHILD)
    tensor_rank = lax.axis_index("tensor")
    child_count = lax.axis_size(CHILD)
    tensor_count = lax.axis_size("tensor")
    kv_local = elite_project.shape[2]
    width_in = elite_project.shape[3]
    width_out = elite_output.shape[3]
    count_rows = tokens.shape[0]
    group_ids = tensor_rank * kv_local + jnp.arange(kv_local, dtype=jnp.int32)
    scale_in = MUTATION / math.sqrt(D)
    scale_out = MUTATION / math.sqrt(KV_HEADS * GROUP * HEAD_DIM)
    out_base = D * KV_HEADS * width_in
    bias_base = out_base + D * KV_HEADS * width_out
    own_seed = mutation_seed[0]
    parent = parent_index[child_rank]
    gathered_in = lax.all_gather(elite_project, CHILD, axis=1, tiled=True)
    arrived_in = lax.dynamic_index_in_dim(gathered_in, parent, 0, keepdims=False)

    shuffled = shuffle_output_rows(elite_output, child_count, tensor_count)
    stage = ring_gather(shuffled, "cz", side)
    stage = ring_gather(stage, "cy", side)
    last_stage_input = stage
    piece = stage.shape[3]
    offsets = jnp.arange(side, dtype=jnp.int32)
    out_rows = child_count * piece

    every_row = jnp.arange(D, dtype=jnp.int32)
    child_in = (
        arrived_in.astype(jnp.float32)
        + scale_in * gaussian(own_seed, counter_grid(every_row, group_ids, width_in, 0))
    ).astype(jnp.bfloat16)
    all_groups = jnp.arange(KV_HEADS, dtype=jnp.int32)
    counter_bias = (
        bias_base + group_ids[:, None] * width_in + jnp.arange(width_in, dtype=jnp.int32)[None, :]
    )
    child_bias = elite_bias[parent] + BIAS_MUTATION * gaussian(own_seed, counter_bias)
    projected = (
        jnp.einsum("rd,dgc->rgc", tokens, child_in, preferred_element_type=jnp.float32)
        + child_bias[None]
    )
    pieces, projected = ring_gather(last_stage_input, "cx", side, hold=projected)
    allowed, cosine, sine_table = episode_tables(episode[0])
    query_part = projected[:, :, : GROUP * HEAD_DIM].reshape(count_rows, kv_local, GROUP, HEAD_DIM)
    key_part = projected[:, :, GROUP * HEAD_DIM : (GROUP + 1) * HEAD_DIM]
    value_part = projected[:, :, (GROUP + 1) * HEAD_DIM :]
    queries = rotary(query_part, cosine[:, None, None, :], sine_table[:, None, None, :]).astype(
        jnp.bfloat16
    )
    key_rows = rotary(key_part, cosine[:, None, :], sine_table[:, None, :]).astype(jnp.bfloat16)
    values = value_part.astype(jnp.bfloat16)
    scores = jnp.einsum("rgqh,sgh->gqrs", queries, key_rows, preferred_element_type=jnp.float32) * (
        1.0 / math.sqrt(HEAD_DIM)
    )
    masked = jnp.where(allowed[None, None], scores, -jnp.inf)
    row_max = jnp.max(masked, axis=-1, keepdims=True)
    weights = jnp.exp(masked - row_max)
    probability = (weights / jnp.sum(weights, axis=-1, keepdims=True)).astype(jnp.bfloat16)
    context = jnp.einsum(
        "gqrs,sgh->rgqh", probability, values, preferred_element_type=jnp.float32
    ).astype(jnp.bfloat16)
    context = context.reshape(count_rows, width_out)
    around = ring_gather(context, "tensor", tensor_count)
    every_context = jnp.take(around, (all_groups - tensor_rank) % tensor_count, axis=0)
    parts = []
    for dx, first, part in pieces:
        picked = lax.dynamic_index_in_dim(part, parent, 2, keepdims=False)
        count_dy = picked.shape[0]
        part_child = (
            ((cx + dx) % side) * (side * side)
            + ((cz + offsets[None, :]) % side) * side
            + (cy + first + jnp.arange(count_dy, dtype=jnp.int32)[:, None]) % side
        ).reshape(-1)
        part_rows = tensor_rank * out_rows + (
            part_child[:, None] * piece + jnp.arange(piece, dtype=jnp.int32)[None, :]
        ).reshape(-1)
        part_out = (
            picked.reshape(-1, KV_HEADS, width_out).astype(jnp.float32)
            + scale_out
            * gaussian(own_seed, counter_grid(part_rows, all_groups, width_out, out_base))
        ).astype(jnp.bfloat16)
        parts.append(
            jnp.einsum(
                "grc,dgc->rd", every_context, part_out, preferred_element_type=jnp.float32
            ).astype(jnp.bfloat16)
        )
    shuffled_attended = jnp.concatenate(parts, axis=1)
    cxs = jnp.arange(child_count, dtype=jnp.int32) // (side * side)
    czs = (jnp.arange(child_count, dtype=jnp.int32) // side) % side
    cys = jnp.arange(child_count, dtype=jnp.int32) % side
    block_of = (
        ((cxs - cx) % side) * (side * side) + ((cys - cy) % side) * side + (czs - cz) % side
    )
    blocks = shuffled_attended.reshape(count_rows, child_count, piece)
    return jnp.take(blocks, block_of, axis=1).reshape(count_rows, out_rows)


def solution(mesh):
    side = round(mesh.shape["child"] ** (1.0 / 3.0))
    fine = jax.sharding.Mesh(
        mesh.devices.reshape(side, side, side, mesh.shape["tensor"]), CHILD + ("tensor",)
    )
    in_specs = (
        P(CHILD, None),
        P(CHILD, None),
        P(),
        P(CHILD),
        P(None, CHILD, "tensor", None),
        P(None, CHILD, "tensor", None),
        P(None, "tensor", None),
    )
    out_specs = P(CHILD, "tensor")
    return jax.shard_map(
        on_device, mesh=fine, in_specs=in_specs, out_specs=out_specs, check_vma=False
    )
```

```python
import math

import jax
import jax.numpy as jnp
from jax import lax
from jax.sharding import PartitionSpec as P

D = 5120
HEAD_DIM = 128
KV_HEADS = 4
GROUP = 5


MUTATION = 0.25
BIAS_MUTATION = 0.05
ROPE_BASE = 1000000.0
NOISE_SPREAD = 147.80054


def mix_hash(seed_value, counter):
    hashed = counter + seed_value * jnp.int32(-1640531535)
    hashed = hashed ^ lax.shift_right_logical(hashed, jnp.full_like(hashed, 16))
    hashed = hashed * jnp.int32(-2048144789)
    hashed = hashed ^ lax.shift_right_logical(hashed, jnp.full_like(hashed, 13))
    hashed = hashed * jnp.int32(-1028477387)
    return hashed ^ lax.shift_right_logical(hashed, jnp.full_like(hashed, 16))


def gaussian(seed_value, counter):
    hashed = mix_hash(seed_value, counter)
    summed = jnp.bitwise_and(hashed, 255)
    summed = summed + jnp.bitwise_and(
        lax.shift_right_logical(hashed, jnp.full_like(hashed, 8)), 255
    )
    summed = summed + jnp.bitwise_and(
        lax.shift_right_logical(hashed, jnp.full_like(hashed, 16)), 255
    )
    summed = summed + lax.shift_right_logical(hashed, jnp.full_like(hashed, 24))
    return (summed - 510).astype(jnp.float32) / NOISE_SPREAD


def counter_grid(row_ids, group_ids, width, base):
    column_ids = jnp.arange(width, dtype=jnp.int32)
    return (
        base
        + (row_ids[:, None, None] * KV_HEADS + group_ids[None, :, None]) * width
        + column_ids[None, None, :]
    )


def rotary(vectors, cosine, sine_table):
    half_dim = vectors.shape[-1] // 2
    first_half = vectors[..., :half_dim]
    second_half = vectors[..., half_dim:]
    return jnp.concatenate(
        [
            first_half * cosine - second_half * sine_table,
            second_half * cosine + first_half * sine_table,
        ],
        axis=-1,
    )


def episode_tables(episode_row):
    count_rows = episode_row.shape[0]
    same_episode = episode_row[:, None] == episode_row[None, :]
    earlier = jnp.sum((episode_row[None, :] < episode_row[:, None]).astype(jnp.int32), axis=1)
    position = jnp.arange(count_rows, dtype=jnp.int32) - earlier
    causal = jnp.arange(count_rows)[None, :] <= jnp.arange(count_rows)[:, None]
    allowed = same_episode & causal
    frequency = jnp.exp(
        jnp.arange(0, HEAD_DIM, 2).astype(jnp.float32) * (-math.log(ROPE_BASE) / HEAD_DIM)
    )
    angles = position.astype(jnp.float32)[:, None] * frequency[None, :]
    return (allowed, jnp.cos(angles), jnp.sin(angles))


CHILD = ("cx", "cz", "cy")


def ring_gather(block, axis_name, size, hold=None):
    forward = [(j, (j + 1) % size) for j in range(size)]
    backward = [(j, (j - 1) % size) for j in range(size)]
    half = block.shape[0] // 2
    if hold is not None:
        prev_low = lax.ppermute(block[:half], axis_name, forward)
        prev_high = lax.ppermute(block[half:], axis_name, forward)
        next_low = lax.ppermute(block[:half], axis_name, backward)
        next_high = lax.ppermute(block[half:], axis_name, backward)
        prev_low, prev_high, next_low, next_high, hold = lax.optimization_barrier(
            (prev_low, prev_high, next_low, next_high, hold)
        )
        far_low = lax.ppermute(prev_low, axis_name, forward)
        far_high = lax.ppermute(next_high, axis_name, backward)
        pieces = [(0, 0, block), (1, 0, next_low), (1, half, next_high), (2, 0, far_low),
                  (2, half, far_high), (3, 0, prev_low), (3, half, prev_high)]
        return pieces, hold
    from_prev = lax.ppermute(block, axis_name, forward)
    from_next = lax.ppermute(block, axis_name, backward)
    far_low = lax.ppermute(from_prev[:half], axis_name, forward)
    far_high = lax.ppermute(from_next[half:], axis_name, backward)
    far = jnp.concatenate([far_low, far_high], axis=0)
    return jnp.stack([block, from_next, far, from_prev])


def shuffle_output_rows(elite_output, child_count, tensor_count):
    local_rows = elite_output.shape[1]
    every_group = lax.all_gather(elite_output, "tensor", axis=2, tiled=True)
    span = child_count // tensor_count
    piece = local_rows // tensor_count
    pairs = []
    for source_child in range(child_count):
        for part in range(tensor_count):
            target_child = tensor_count * (source_child % span) + part
            target_tensor = source_child // span
            pairs.append(
                (source_child * tensor_count + part, target_child * tensor_count + target_tensor)
            )
    tensor_rank = lax.axis_index("tensor")
    mine = lax.dynamic_slice_in_dim(every_group, tensor_rank * piece, piece, axis=1)
    return lax.ppermute(mine, CHILD + ("tensor",), pairs)


def on_device(
    tokens, episode, parent_index, mutation_seed, elite_project, elite_output, elite_bias
):
    side = lax.axis_size("cx")
    cx, cz, cy = (lax.axis_index(name) for name in CHILD)
    child_rank = lax.axis_index(CHILD)
    tensor_rank = lax.axis_index("tensor")
    child_count = lax.axis_size(CHILD)
    tensor_count = lax.axis_size("tensor")
    kv_local = elite_project.shape[2]
    width_in = elite_project.shape[3]
    width_out = elite_output.shape[3]
    count_rows = tokens.shape[0]
    group_ids = tensor_rank * kv_local + jnp.arange(kv_local, dtype=jnp.int32)
    scale_in = MUTATION / math.sqrt(D)
    scale_out = MUTATION / math.sqrt(KV_HEADS * GROUP * HEAD_DIM)
    out_base = D * KV_HEADS * width_in
    bias_base = out_base + D * KV_HEADS * width_out
    own_seed = mutation_seed[0]
    parent = parent_index[child_rank]
    gathered_in = lax.all_gather(elite_project, CHILD, axis=1, tiled=True)
    arrived_in = lax.dynamic_index_in_dim(gathered_in, parent, 0, keepdims=False)

    shuffled = shuffle_output_rows(elite_output, child_count, tensor_count)
    stage = ring_gather(shuffled, "cz", side)
    stage = ring_gather(stage, "cy", side)
    last_stage_input = stage
    piece = stage.shape[3]
    offsets = jnp.arange(side, dtype=jnp.int32)
    out_rows = child_count * piece

    every_row = jnp.arange(D, dtype=jnp.int32)
    child_in = (
        arrived_in.astype(jnp.float32)
        + scale_in * gaussian(own_seed, counter_grid(every_row, group_ids, width_in, 0))
    ).astype(jnp.bfloat16)
    all_groups = jnp.arange(KV_HEADS, dtype=jnp.int32)
    counter_bias = (
        bias_base + group_ids[:, None] * width_in + jnp.arange(width_in, dtype=jnp.int32)[None, :]
    )
    child_bias = elite_bias[parent] + BIAS_MUTATION * gaussian(own_seed, counter_bias)
    projected = (
        jnp.einsum("rd,dgc->rgc", tokens, child_in, preferred_element_type=jnp.float32)
        + child_bias[None]
    )
    pieces, projected = ring_gather(last_stage_input, "cx", side, hold=projected)
    allowed, cosine, sine_table = episode_tables(episode[0])
    query_part = projected[:, :, : GROUP * HEAD_DIM].reshape(count_rows, kv_local, GROUP, HEAD_DIM)
    key_part = projected[:, :, GROUP * HEAD_DIM : (GROUP + 1) * HEAD_DIM]
    value_part = projected[:, :, (GROUP + 1) * HEAD_DIM :]
    queries = rotary(query_part, cosine[:, None, None, :], sine_table[:, None, None, :]).astype(
        jnp.bfloat16
    )
    key_rows = rotary(key_part, cosine[:, None, :], sine_table[:, None, :]).astype(jnp.bfloat16)
    values = value_part.astype(jnp.bfloat16)
    scores = jnp.einsum("rgqh,sgh->gqrs", queries, key_rows, preferred_element_type=jnp.float32) * (
        1.0 / math.sqrt(HEAD_DIM)
    )
    masked = jnp.where(allowed[None, None], scores, -jnp.inf)
    row_max = jnp.max(masked, axis=-1, keepdims=True)
    weights = jnp.exp(masked - row_max)
    probability = (weights / jnp.sum(weights, axis=-1, keepdims=True)).astype(jnp.bfloat16)
    context = jnp.einsum(
        "gqrs,sgh->rgqh", probability, values, preferred_element_type=jnp.float32
    ).astype(jnp.bfloat16)
    context = context.reshape(count_rows, width_out)
    around = ring_gather(context, "tensor", tensor_count)
    every_context = jnp.take(around, (all_groups - tensor_rank) % tensor_count, axis=0)
    parts = []
    for dx, first, part in pieces:
        picked = lax.dynamic_index_in_dim(part, parent, 2, keepdims=False)
        count_dy = picked.shape[0]
        part_child = (
            ((cx + dx) % side) * (side * side)
            + ((cz + offsets[None, :]) % side) * side
            + (cy + first + jnp.arange(count_dy, dtype=jnp.int32)[:, None]) % side
        ).reshape(-1)
        part_rows = tensor_rank * out_rows + (
            part_child[:, None] * piece + jnp.arange(piece, dtype=jnp.int32)[None, :]
        ).reshape(-1)
        part_out = (
            picked.reshape(-1, KV_HEADS, width_out).astype(jnp.float32)
            + scale_out
            * gaussian(own_seed, counter_grid(part_rows, all_groups, width_out, out_base))
        ).astype(jnp.bfloat16)
        parts.append(
            jnp.einsum(
                "grc,dgc->rd", every_context, part_out, preferred_element_type=jnp.float32
            ).astype(jnp.bfloat16)
        )
    shuffled_attended = jnp.concatenate(parts, axis=1)
    cxs = jnp.arange(child_count, dtype=jnp.int32) // (side * side)
    czs = (jnp.arange(child_count, dtype=jnp.int32) // side) % side
    cys = jnp.arange(child_count, dtype=jnp.int32) % side
    block_of = (
        ((cxs - cx) % side) * (side * side) + ((cys - cy) % side) * side + (czs - cz) % side
    )
    blocks = shuffled_attended.reshape(count_rows, child_count, piece)
    return jnp.take(blocks, block_of, axis=1).reshape(count_rows, out_rows)


def solution(mesh):
    side = round(mesh.shape["child"] ** (1.0 / 3.0))
    fine = jax.sharding.Mesh(
        mesh.devices.reshape(side, side, side, mesh.shape["tensor"]), CHILD + ("tensor",)
    )
    in_specs = (
        P(CHILD, None),
        P(CHILD, None),
        P(),
        P(CHILD),
        P(None, CHILD, "tensor", None),
        P(None, CHILD, "tensor", None),
        P(None, "tensor", None),
    )
    out_specs = P(CHILD, "tensor")
    return jax.shard_map(
        on_device, mesh=fine, in_specs=in_specs, out_specs=out_specs, check_vma=False
    )
```

```python
import math

import jax
import jax.numpy as jnp
from jax import lax
from jax.sharding import PartitionSpec as P

D = 5120
HEAD_DIM = 128
KV_HEADS = 4
GROUP = 5


MUTATION = 0.25
BIAS_MUTATION = 0.05
ROPE_BASE = 1000000.0
NOISE_SPREAD = 147.80054


def mix_hash(seed_value, counter):
    hashed = counter + seed_value * jnp.int32(-1640531535)
    hashed = hashed ^ lax.shift_right_logical(hashed, jnp.full_like(hashed, 16))
    hashed = hashed * jnp.int32(-2048144789)
    hashed = hashed ^ lax.shift_right_logical(hashed, jnp.full_like(hashed, 13))
    hashed = hashed * jnp.int32(-1028477387)
    return hashed ^ lax.shift_right_logical(hashed, jnp.full_like(hashed, 16))


def gaussian(seed_value, counter):
    hashed = mix_hash(seed_value, counter)
    summed = jnp.bitwise_and(hashed, 255)
    summed = summed + jnp.bitwise_and(
        lax.shift_right_logical(hashed, jnp.full_like(hashed, 8)), 255
    )
    summed = summed + jnp.bitwise_and(
        lax.shift_right_logical(hashed, jnp.full_like(hashed, 16)), 255
    )
    summed = summed + lax.shift_right_logical(hashed, jnp.full_like(hashed, 24))
    return (summed - 510).astype(jnp.float32) / NOISE_SPREAD


def counter_grid(row_ids, group_ids, width, base):
    column_ids = jnp.arange(width, dtype=jnp.int32)
    return (
        base
        + (row_ids[:, None, None] * KV_HEADS + group_ids[None, :, None]) * width
        + column_ids[None, None, :]
    )


def rotary(vectors, cosine, sine_table):
    half_dim = vectors.shape[-1] // 2
    first_half = vectors[..., :half_dim]
    second_half = vectors[..., half_dim:]
    return jnp.concatenate(
        [
            first_half * cosine - second_half * sine_table,
            second_half * cosine + first_half * sine_table,
        ],
        axis=-1,
    )


def episode_tables(episode_row):
    count_rows = episode_row.shape[0]
    same_episode = episode_row[:, None] == episode_row[None, :]
    earlier = jnp.sum((episode_row[None, :] < episode_row[:, None]).astype(jnp.int32), axis=1)
    position = jnp.arange(count_rows, dtype=jnp.int32) - earlier
    causal = jnp.arange(count_rows)[None, :] <= jnp.arange(count_rows)[:, None]
    allowed = same_episode & causal
    frequency = jnp.exp(
        jnp.arange(0, HEAD_DIM, 2).astype(jnp.float32) * (-math.log(ROPE_BASE) / HEAD_DIM)
    )
    angles = position.astype(jnp.float32)[:, None] * frequency[None, :]
    return (allowed, jnp.cos(angles), jnp.sin(angles))


CHILD = ("cx", "cz", "cy")


def ring_gather(block, axis_name, size, hold=None):
    forward = [(j, (j + 1) % size) for j in range(size)]
    backward = [(j, (j - 1) % size) for j in range(size)]
    from_prev = lax.ppermute(block, axis_name, forward)
    from_next = lax.ppermute(block, axis_name, backward)
    if hold is not None:
        from_prev, from_next, hold = lax.optimization_barrier((from_prev, from_next, hold))
    half = block.shape[0] // 2
    onward_low, onward_high = from_prev[:half], from_next[half:]
    if hold is not None:
        onward_low, onward_high, hold = lax.optimization_barrier(
            (onward_low, onward_high, hold)
        )
    far_low = lax.ppermute(onward_low, axis_name, forward)
    far_high = lax.ppermute(onward_high, axis_name, backward)
    if hold is not None:
        pieces = [(0, 0, block), (1, 0, from_next), (2, 0, far_low), (2, half, far_high),
                  (3, 0, from_prev)]
        return pieces, hold
    far = jnp.concatenate([far_low, far_high], axis=0)
    return jnp.stack([block, from_next, far, from_prev])


def shuffle_output_rows(elite_output, child_count, tensor_count):
    local_rows = elite_output.shape[1]
    every_group = lax.all_gather(elite_output, "tensor", axis=2, tiled=True)
    span = child_count // tensor_count
    piece = local_rows // tensor_count
    pairs = []
    for source_child in range(child_count):
        for part in range(tensor_count):
            target_child = tensor_count * (source_child % span) + part
            target_tensor = source_child // span
            pairs.append(
                (source_child * tensor_count + part, target_child * tensor_count + target_tensor)
            )
    tensor_rank = lax.axis_index("tensor")
    mine = lax.dynamic_slice_in_dim(every_group, tensor_rank * piece, piece, axis=1)
    return lax.ppermute(mine, CHILD + ("tensor",), pairs)


def on_device(
    tokens, episode, parent_index, mutation_seed, elite_project, elite_output, elite_bias
):
    side = lax.axis_size("cx")
    cx, cz, cy = (lax.axis_index(name) for name in CHILD)
    child_rank = lax.axis_index(CHILD)
    tensor_rank = lax.axis_index("tensor")
    child_count = lax.axis_size(CHILD)
    tensor_count = lax.axis_size("tensor")
    kv_local = elite_project.shape[2]
    width_in = elite_project.shape[3]
    width_out = elite_output.shape[3]
    count_rows = tokens.shape[0]
    group_ids = tensor_rank * kv_local + jnp.arange(kv_local, dtype=jnp.int32)
    scale_in = MUTATION / math.sqrt(D)
    scale_out = MUTATION / math.sqrt(KV_HEADS * GROUP * HEAD_DIM)
    out_base = D * KV_HEADS * width_in
    bias_base = out_base + D * KV_HEADS * width_out
    own_seed = mutation_seed[0]
    parent = parent_index[child_rank]
    gathered_in = lax.all_gather(elite_project, CHILD, axis=1, tiled=True)
    arrived_in = lax.dynamic_index_in_dim(gathered_in, parent, 0, keepdims=False)

    shuffled = shuffle_output_rows(elite_output, child_count, tensor_count)
    stage = ring_gather(shuffled, "cz", side)
    stage = ring_gather(stage, "cy", side)
    last_stage_input = stage
    piece = stage.shape[3]
    offsets = jnp.arange(side, dtype=jnp.int32)
    out_rows = child_count * piece

    every_row = jnp.arange(D, dtype=jnp.int32)
    child_in = (
        arrived_in.astype(jnp.float32)
        + scale_in * gaussian(own_seed, counter_grid(every_row, group_ids, width_in, 0))
    ).astype(jnp.bfloat16)
    all_groups = jnp.arange(KV_HEADS, dtype=jnp.int32)
    counter_bias = (
        bias_base + group_ids[:, None] * width_in + jnp.arange(width_in, dtype=jnp.int32)[None, :]
    )
    child_bias = elite_bias[parent] + BIAS_MUTATION * gaussian(own_seed, counter_bias)
    projected = (
        jnp.einsum("rd,dgc->rgc", tokens, child_in, preferred_element_type=jnp.float32)
        + child_bias[None]
    )
    pieces, projected = ring_gather(last_stage_input, "cx", side, hold=projected)
    allowed, cosine, sine_table = episode_tables(episode[0])
    query_part = projected[:, :, : GROUP * HEAD_DIM].reshape(count_rows, kv_local, GROUP, HEAD_DIM)
    key_part = projected[:, :, GROUP * HEAD_DIM : (GROUP + 1) * HEAD_DIM]
    value_part = projected[:, :, (GROUP + 1) * HEAD_DIM :]
    queries = rotary(query_part, cosine[:, None, None, :], sine_table[:, None, None, :]).astype(
        jnp.bfloat16
    )
    key_rows = rotary(key_part, cosine[:, None, :], sine_table[:, None, :]).astype(jnp.bfloat16)
    values = value_part.astype(jnp.bfloat16)
    scores = jnp.einsum("rgqh,sgh->gqrs", queries, key_rows, preferred_element_type=jnp.float32) * (
        1.0 / math.sqrt(HEAD_DIM)
    )
    masked = jnp.where(allowed[None, None], scores, -jnp.inf)
    row_max = jnp.max(masked, axis=-1, keepdims=True)
    weights = jnp.exp(masked - row_max)
    probability = (weights / jnp.sum(weights, axis=-1, keepdims=True)).astype(jnp.bfloat16)
    context = jnp.einsum(
        "gqrs,sgh->rgqh", probability, values, preferred_element_type=jnp.float32
    ).astype(jnp.bfloat16)
    context = context.reshape(count_rows, width_out)
    around = ring_gather(context, "tensor", tensor_count)
    every_context = jnp.take(around, (all_groups - tensor_rank) % tensor_count, axis=0)
    parts = []
    for dx, first, part in pieces:
        picked = lax.dynamic_index_in_dim(part, parent, 2, keepdims=False)
        count_dy = picked.shape[0]
        part_child = (
            ((cx + dx) % side) * (side * side)
            + ((cz + offsets[None, :]) % side) * side
            + (cy + first + jnp.arange(count_dy, dtype=jnp.int32)[:, None]) % side
        ).reshape(-1)
        part_rows = tensor_rank * out_rows + (
            part_child[:, None] * piece + jnp.arange(piece, dtype=jnp.int32)[None, :]
        ).reshape(-1)
        part_out = (
            picked.reshape(-1, KV_HEADS, width_out).astype(jnp.float32)
            + scale_out
            * gaussian(own_seed, counter_grid(part_rows, all_groups, width_out, out_base))
        ).astype(jnp.bfloat16)
        parts.append(
            jnp.einsum(
                "grc,dgc->rd", every_context, part_out, preferred_element_type=jnp.float32
            ).astype(jnp.bfloat16)
        )
    shuffled_attended = jnp.concatenate(parts, axis=1)
    cxs = jnp.arange(child_count, dtype=jnp.int32) // (side * side)
    czs = (jnp.arange(child_count, dtype=jnp.int32) // side) % side
    cys = jnp.arange(child_count, dtype=jnp.int32) % side
    block_of = (
        ((cxs - cx) % side) * (side * side) + ((cys - cy) % side) * side + (czs - cz) % side
    )
    blocks = shuffled_attended.reshape(count_rows, child_count, piece)
    return jnp.take(blocks, block_of, axis=1).reshape(count_rows, out_rows)


def solution(mesh):
    side = round(mesh.shape["child"] ** (1.0 / 3.0))
    fine = jax.sharding.Mesh(
        mesh.devices.reshape(side, side, side, mesh.shape["tensor"]), CHILD + ("tensor",)
    )
    in_specs = (
        P(CHILD, None),
        P(CHILD, None),
        P(),
        P(CHILD),
        P(None, CHILD, "tensor", None),
        P(None, CHILD, "tensor", None),
        P(None, "tensor", None),
    )
    out_specs = P(CHILD, "tensor")
    return jax.shard_map(
        on_device, mesh=fine, in_specs=in_specs, out_specs=out_specs, check_vma=False
    )
```
